256 devices in a mesh: blk: 8 (over x, core), dev: 32 (over z, y).
Axes of the slice: x: 4, y: 4, z: 8, core: 2. Of those that a mesh axis runs over, the one named last changes fastest.
Arguments:
- echoes: bfloat16 [2, 4, 2048, 16384], P(None, None, ('blk', 'dev')), may hold values from -6 to 6
- range_phase: float32 [16384], replicated, may hold values from -3.140625 to 3.140625
- offsets: int32 [16384], P('dev'), may hold values from 0 to 56, as said below
- tap_weights: float32 [8, 384], replicated, may hold values from -2 to 2
- channel_mix: float32 [2, 4, 4, 384], replicated, may hold values from -2 to 2
- azimuth_filter: float32 [2, 4, 384], replicated, may hold values from -4 to 4
Outputs:
- focused_image: bfloat16 [2, 4, 2048, 16384], P(None, None, 'blk', 'dev')
The draws below stay inside these ranges and needn't reach their ends.
Inputs may be any that keep to these rules, and one draw needn't show every extreme that they name: `offsets`: each range bin's offset lies between 0 and 56; some range bin has exactly 56.
All inputs are finite; a program needn't handle non-finite values.
Results may differ from the reference program's by a relative error of at most 0.0088.
Values may be sent and summed in bfloat16 or wider, within the bound.
No kernel may reach another device: no remote copies, remote signals or barrier semaphores. Data moves between devices by JAX's collectives and lax.ppermute only.
A program may use at most 128 MiB of HBM per device.

```python
import math
import jax
import jax.numpy as jnp
from jax import lax

NR = 16384
R1 = 128
R2 = 128
CH = 4
TAPS = 8
MARG = 64
GROUP_P = 256
INTERSECTION = 128
WINDOW = 384
PULSES = 2048
N_BLK = 8


def draw_offsets(key, part):
    values = jax.random.randint(jax.random.fold_in(key, 11), (NR,), 0, MARG - TAPS + 1)
    spots = jax.random.randint(jax.random.fold_in(key, 12), (2,), 0, NR)
    values = values.at[spots[0]].set(0)
    values = values.at[spots[1]].set(MARG - TAPS)
    return values.astype(jnp.int32)


def shard_levels(stream_key, extent, shards, low, top_value):
    def one(dim, shards_of):
        draws = jax.random.uniform(jax.random.fold_in(jax.random.fold_in(stream_key, 6), dim), (shards_of,), jnp.float32, low / len(shards), top_value / len(shards))
        return jnp.repeat(jnp.exp(draws), extent[dim] // shards_of).reshape((-1,) + (1,) * (len(extent) - dim - 1))

    gain = one(*shards[0])
    for cut in shards[1:]:
        gain = gain * one(*cut)
    return gain


def scatter_about(stream_key, dims, spread, limit, cuts=(), held_as=jnp.bfloat16):
    result = jax.random.normal(stream_key, dims, jnp.float32) * spread
    if len(cuts) > 0:
        result = shard_levels(stream_key, dims, cuts, -0.22, 0.18) * result
    return jnp.clip(result, min=-limit, max=limit).astype(held_as)


def setup_inputs(seed: int = 0) -> dict:
    seeds = jax.random.split(jax.random.key(seed), 7)
    echoes = scatter_about(seeds[0], (2, CH, PULSES, NR), 1.0, 6.0, ((2, 256),))
    range_phase = jnp.clip(jax.random.uniform(seeds[1], (NR,), jnp.float32, -3.140625, 3.140625), -3.140625, 3.140625)
    offsets = draw_offsets(jax.random.fold_in(seeds[6], 71), 0)
    tap_weights = scatter_about(seeds[3], (TAPS, WINDOW), TAPS ** -0.5, 2.0, (), jnp.float32)
    channel_mix = scatter_about(seeds[4], (2, CH, CH, WINDOW), 0.35, 2.0, (), jnp.float32)
    azimuth_filter = scatter_about(seeds[5], (2, CH, WINDOW), 0.7, 4.0, (), jnp.float32)
    return dict(echoes=echoes, range_phase=range_phase, offsets=offsets, tap_weights=tap_weights, channel_mix=channel_mix, azimuth_filter=azimuth_filter)


def phase_pair(row_count, col_count, length, direction, factor):
    product = jnp.arange(row_count, dtype=jnp.int32)[:, None] * jnp.arange(col_count, dtype=jnp.int32)[None, :] % length
    angle = product.astype(jnp.float32) * (direction * 2.0 * math.pi / length)
    return (jnp.cos(angle) * factor, jnp.sin(angle) * factor)

def settle(values):
    return lax.optimization_barrier(values.astype(jnp.bfloat16)).astype(jnp.float32)

def rounded_pair(row_count, col_count, length, direction, factor):
    cosine, sine = phase_pair(row_count, col_count, length, direction, factor)
    return (settle(cosine), settle(sine))

def compress(echo, range_phase):
    cosine = jnp.cos(range_phase)
    sine = jnp.sin(range_phase)
    real_in = echo[0].astype(jnp.float32)
    imag_in = echo[1].astype(jnp.float32)
    spec_real = settle(real_in * cosine - imag_in * sine)
    spec_imag = settle(real_in * sine + imag_in * cosine)
    leading_shape = spec_real.shape[:-1]
    spec_real = spec_real.reshape(leading_shape + (R1, R2))
    spec_imag = spec_imag.reshape(leading_shape + (R1, R2))
    first_re, first_im = rounded_pair(R1, R1, R1, 1.0, 1.0)
    section_real = jnp.einsum('nj,cqjb->cqnb', first_re, spec_real) - jnp.einsum('nj,cqjb->cqnb', first_im, spec_imag)
    section_imag = jnp.einsum('nj,cqjb->cqnb', first_re, spec_imag) + jnp.einsum('nj,cqjb->cqnb', first_im, spec_real)
    twist_re, twist_im = phase_pair(R1, R2, NR, 1.0, 1.0 / math.sqrt(NR))
    part_real = settle(section_real * twist_re - section_imag * twist_im)
    part_imag = settle(section_real * twist_im + section_imag * twist_re)
    second_re, second_im = rounded_pair(R2, R2, R2, 1.0, 1.0)
    out_real = jnp.einsum('cqnb,bm->cqmn', part_real, second_re) - jnp.einsum('cqnb,bm->cqmn', part_imag, second_im)
    out_imag = jnp.einsum('cqnb,bm->cqmn', part_real, second_im) + jnp.einsum('cqnb,bm->cqmn', part_imag, second_re)
    return jnp.stack([out_real, out_imag]).reshape((2,) + leading_shape + (NR,)).astype(jnp.bfloat16)

def focus(window, offsets, tap_weights, channel_mix, azimuth_filter):
    fwd_re, fwd_im = rounded_pair(WINDOW, WINDOW, WINDOW, -1.0, 1.0 / math.sqrt(WINDOW))
    win_real = window[0].astype(jnp.float32)
    win_imag = window[1].astype(jnp.float32)
    dop_real = jnp.einsum('fw,cwr->crf', fwd_re, win_real) - jnp.einsum('fw,cwr->crf', fwd_im, win_imag)
    dop_imag = jnp.einsum('fw,cwr->crf', fwd_re, win_imag) + jnp.einsum('fw,cwr->crf', fwd_im, win_real)
    dop_real = settle(dop_real)
    dop_imag = settle(dop_imag)
    tail = jnp.zeros((CH, MARG, WINDOW), jnp.float32)
    ext_real = jnp.concatenate([dop_real, tail], axis=1)
    ext_imag = jnp.concatenate([dop_imag, tail], axis=1)
    moved_real = jnp.zeros((CH, NR, WINDOW), jnp.float32)
    moved_imag = jnp.zeros((CH, NR, WINDOW), jnp.float32)
    start_rows = jnp.arange(NR, dtype=jnp.int32) + offsets.astype(jnp.int32)
    for tap_index in range(TAPS):
        chosen = (start_rows + tap_index).astype(jnp.int32)
        moved_real = moved_real + jnp.take(ext_real, chosen, axis=1) * tap_weights[tap_index]
        moved_imag = moved_imag + jnp.take(ext_imag, chosen, axis=1) * tap_weights[tap_index]
    rows_real = []
    rows_imag = []
    for channel in range(CH):
        sum_real = jnp.zeros((NR, WINDOW), jnp.float32)
        sum_imag = jnp.zeros((NR, WINDOW), jnp.float32)
        for other_chan in range(CH):
            coef_real = channel_mix[0, channel, other_chan]
            coef_imag = channel_mix[1, channel, other_chan]
            sum_real = sum_real + coef_real * moved_real[other_chan] - coef_imag * moved_imag[other_chan]
            sum_imag = sum_imag + coef_real * moved_imag[other_chan] + coef_imag * moved_real[other_chan]
        filt_real = azimuth_filter[0, channel]
        filt_imag = azimuth_filter[1, channel]
        rows_real.append(filt_real * sum_real - filt_imag * sum_imag)
        rows_imag.append(filt_real * sum_imag + filt_imag * sum_real)
    foc_real = settle(jnp.stack(rows_real))
    foc_imag = settle(jnp.stack(rows_imag))
    back_re, back_im = rounded_pair(GROUP_P, WINDOW, WINDOW, 1.0, 1.0 / math.sqrt(WINDOW))
    img_real = jnp.einsum('pf,crf->cpr', back_re, foc_real) - jnp.einsum('pf,crf->cpr', back_im, foc_imag)
    img_imag = jnp.einsum('pf,crf->cpr', back_re, foc_imag) + jnp.einsum('pf,crf->cpr', back_im, foc_real)
    return jnp.stack([img_real, img_imag]).astype(jnp.bfloat16)

def reference(echoes, range_phase, offsets, tap_weights, channel_mix, azimuth_filter):
    grouped = echoes.reshape(2, CH, N_BLK, GROUP_P, NR).transpose(2, 0, 1, 3, 4)
    compressed = lax.map(lambda group: compress(group, range_phase), grouped)
    following = jnp.concatenate([compressed[1:, :, :, :INTERSECTION], jnp.zeros_like(compressed[:1, :, :, :INTERSECTION])], axis=0)
    windows = jnp.concatenate([compressed, following], axis=3)
    images = lax.map(lambda group: focus(group, offsets, tap_weights, channel_mix, azimuth_filter), windows)
    return images.transpose(1, 2, 0, 3, 4).reshape(2, CH, PULSES, NR)
```

```python
import math

import jax
import jax.numpy as jnp
from jax import lax
from jax.sharding import PartitionSpec as P

R1 = 128
MARG = 64


def shifted(block, axis, distance):
    devices = range(lax.axis_size(axis))
    route = [(i - distance, i) for i in devices if i - distance in devices]
    return lax.ppermute(block, axis, route)


def phase_pair(row_count, col_count, length, direction, factor):
    product = (
        jnp.arange(row_count, dtype=jnp.int32)[:, None]
        * jnp.arange(col_count, dtype=jnp.int32)[None, :]
        % length
    )
    angle = product.astype(jnp.float32) * (direction * 2.0 * math.pi / length)
    return (jnp.cos(angle) * factor, jnp.sin(angle) * factor)


def complex_table(row_count, col_count, length, direction, factor):
    cosine, sine = phase_pair(row_count, col_count, length, direction, factor)
    upper = jnp.stack([cosine, -sine], axis=1)
    lower = jnp.stack([sine, cosine], axis=1)
    return jnp.stack([upper, lower]).astype(jnp.bfloat16)


def apply_table(table, data, part_dim, index_dim):
    return lax.dot_general(
        table, data, (((2, 3), (part_dim, index_dim)), ((), ())), preferred_element_type=jnp.float32
    )


def compress(echoes, range_phase):
    cosine = jnp.cos(range_phase)
    sine = jnp.sin(range_phase)
    real_in = echoes[0].astype(jnp.float32)
    imag_in = echoes[1].astype(jnp.float32)
    spectrum = jnp.stack(
        [real_in * cosine - imag_in * sine, real_in * sine + imag_in * cosine]
    ).astype(jnp.bfloat16)
    channels = spectrum.shape[1]
    pulses = spectrum.shape[2]
    range_bins = spectrum.shape[3]
    second = range_bins // R1
    spectrum = spectrum.reshape((2, channels, pulses, R1, second))
    section = apply_table(complex_table(R1, R1, R1, 1.0, 1.0), spectrum, 0, 3)
    twist_re, twist_im = phase_pair(R1, second, range_bins, 1.0, 1.0 / math.sqrt(range_bins))
    twist_re = twist_re[:, None, None, :]
    twist_im = twist_im[:, None, None, :]
    partial_terms = jnp.stack(
        [
            section[0] * twist_re - section[1] * twist_im,
            section[0] * twist_im + section[1] * twist_re,
        ]
    ).astype(jnp.bfloat16)
    result = apply_table(
        complex_table(second, second, second, 1.0, 1.0), partial_terms, 0, 4
    ).astype(jnp.bfloat16)
    return result.transpose(0, 3, 4, 1, 2).reshape((2, channels, pulses, range_bins))


def doppler(window):
    wide = window.shape[2]
    forward = complex_table(wide, wide, wide, -1.0, 1.0 / math.sqrt(wide))
    return apply_table(forward, window, 0, 2).astype(jnp.bfloat16)


def migrate(extended, offsets, tap_weights, block):
    tile = min(128, block)
    taps = tap_weights.shape[0]
    pieces = []
    for tile_index in range(block // tile):
        first = tile_index * tile
        rows_here = jnp.arange(tile, dtype=jnp.int32)
        target = rows_here + offsets[first : first + tile]
        columns = jnp.arange(tile + MARG, dtype=jnp.int32)
        tap_range = jnp.arange(taps, dtype=jnp.int32)
        onehot = (
            columns[None, None, :] == target[None, :, None] + tap_range[:, None, None]
        ).astype(jnp.bfloat16)
        window_part = extended[:, :, :, first : first + tile + MARG]
        picked = lax.dot_general(
            window_part, onehot, (((3,), (2,)), ((), ())), preferred_element_type=jnp.float32
        )
        total = jnp.zeros(picked.shape[:3] + (tile,), jnp.float32)
        for tap_index in range(taps):
            total = total + picked[:, :, :, tap_index] * tap_weights[tap_index][None, :, None, None]
        pieces.append(total)
    return jnp.concatenate(pieces, axis=3)


def body(echoes, range_phase, offsets, tap_weights, channel_mix, azimuth_filter):
    dev_count = lax.axis_size("dev")
    parts, channels, pulses, range_bins = echoes.shape
    second = range_bins // R1
    per_block = second // dev_count
    block = range_bins // dev_count
    cosine = jnp.cos(range_phase)
    sine = jnp.sin(range_phase)
    real_in = echoes[0].astype(jnp.float32)
    imag_in = echoes[1].astype(jnp.float32)
    spectrum = jnp.stack(
        [real_in * cosine - imag_in * sine, real_in * sine + imag_in * cosine]
    ).astype(jnp.bfloat16)
    spectrum = spectrum.reshape((2, channels, pulses, R1, second))
    section = apply_table(complex_table(R1, R1, R1, 1.0, 1.0), spectrum, 0, 3)
    twist_re, twist_im = phase_pair(R1, second, range_bins, 1.0, 1.0 / math.sqrt(range_bins))
    twist_re = twist_re[:, None, None, :]
    twist_im = twist_im[:, None, None, :]
    partial_terms = jnp.stack(
        [
            section[0] * twist_re - section[1] * twist_im,
            section[0] * twist_im + section[1] * twist_re,
        ]
    ).astype(jnp.bfloat16)
    partial_terms = partial_terms.transpose(0, 2, 3, 1, 4)
    second_table = complex_table(second, second, second, 1.0, 1.0).transpose(1, 0, 2, 3)
    second_table = second_table.reshape((dev_count, per_block, 2, 2, second))
    result = lax.dot_general(
        second_table, partial_terms, (((3, 4), (0, 4)), ((), ())), preferred_element_type=jnp.float32
    ).astype(jnp.bfloat16)
    result = result.transpose(0, 2, 3, 4, 1, 5).reshape((dev_count, 2, channels, pulses, block))
    turned = lax.all_to_all(result, "dev", 0, 0, tiled=True)
    group_pulses = dev_count * pulses
    wide = group_pulses + group_pulses // 2
    following = shifted(turned[: dev_count // 2], "blk", -1)
    forward = complex_table(wide, wide, wide, -1.0, 1.0 / math.sqrt(wide))
    own_table = forward[:, :, :, :group_pulses].reshape((2, wide, 2, dev_count, pulses))
    next_table = forward[:, :, :, group_pulses:].reshape((2, wide, 2, dev_count // 2, pulses))
    dims = (((2, 3, 4), (1, 0, 3)), ((), ()))
    spectra = (
        lax.dot_general(own_table, turned, dims, preferred_element_type=jnp.float32)
        + lax.dot_general(next_table, following, dims, preferred_element_type=jnp.float32)
    ).astype(jnp.bfloat16)
    border = shifted(spectra[:, :, :, :MARG], "dev", -1)
    extended = jnp.concatenate([spectra, border], axis=3)
    moved = migrate(extended, offsets, tap_weights, block)
    mix_real = (
        azimuth_filter[0][:, None, :] * channel_mix[0]
        - azimuth_filter[1][:, None, :] * channel_mix[1]
    )
    mix_imag = (
        azimuth_filter[0][:, None, :] * channel_mix[1]
        + azimuth_filter[1][:, None, :] * channel_mix[0]
    )
    rows_real = []
    rows_imag = []
    for channel in range(channels):
        sum_real = jnp.zeros((wide, block), jnp.float32)
        sum_imag = jnp.zeros((wide, block), jnp.float32)
        for other_chan in range(channels):
            coef_real = mix_real[channel, other_chan][:, None]
            coef_imag = mix_imag[channel, other_chan][:, None]
            sum_real = (
                sum_real + coef_real * moved[0, :, other_chan] - coef_imag * moved[1, :, other_chan]
            )
            sum_imag = (
                sum_imag + coef_real * moved[1, :, other_chan] + coef_imag * moved[0, :, other_chan]
            )
        rows_real.append(sum_real)
        rows_imag.append(sum_imag)
    focused = jnp.stack([jnp.stack(rows_real, axis=1), jnp.stack(rows_imag, axis=1)]).astype(
        jnp.bfloat16
    )
    backward = complex_table(group_pulses, wide, wide, 1.0, 1.0 / math.sqrt(wide))
    image = apply_table(backward, focused, 0, 1).astype(jnp.bfloat16)
    return image.transpose(0, 2, 1, 3)


def solution(mesh):
    in_specs = (P(None, None, ("blk", "dev"), None), P(), P("dev"), P(), P(), P())
    out_specs = P(None, None, "blk", "dev")
    return jax.shard_map(body, mesh=mesh, in_specs=in_specs, out_specs=out_specs, check_vma=False)
```

```python
import math

import jax
import jax.numpy as jnp
from jax import lax
from jax.sharding import PartitionSpec as P


R1 = 128
MARG = 64


def shifted(block, axis, distance):
    devices = range(lax.axis_size(axis))
    route = [(i - distance, i) for i in devices if i - distance in devices]
    return lax.ppermute(block, axis, route)


def phase_pair(row_count, col_count, length, direction, factor):
    product = (
        jnp.arange(row_count, dtype=jnp.int32)[:, None]
        * jnp.arange(col_count, dtype=jnp.int32)[None, :]
        % length
    )
    angle = product.astype(jnp.float32) * (direction * 2.0 * math.pi / length)
    return (jnp.cos(angle) * factor, jnp.sin(angle) * factor)


def complex_table(row_count, col_count, length, direction, factor):
    cosine, sine = phase_pair(row_count, col_count, length, direction, factor)
    upper = jnp.stack([cosine, -sine], axis=1)
    lower = jnp.stack([sine, cosine], axis=1)
    return jnp.stack([upper, lower]).astype(jnp.bfloat16)


def apply_table(table, data, part_dim, index_dim):
    return lax.dot_general(
        table, data, (((2, 3), (part_dim, index_dim)), ((), ())), preferred_element_type=jnp.float32
    )


def migrate(extended, offsets, tap_weights, block):
    tile = min(128, block)
    taps = tap_weights.shape[0]
    pieces = []
    for tile_index in range(block // tile):
        first = tile_index * tile
        rows_here = jnp.arange(tile, dtype=jnp.int32)
        target = rows_here + offsets[first : first + tile]
        columns = jnp.arange(tile + MARG, dtype=jnp.int32)
        tap_range = jnp.arange(taps, dtype=jnp.int32)
        onehot = (
            columns[None, None, :] == target[None, :, None] + tap_range[:, None, None]
        ).astype(jnp.bfloat16)
        window_part = extended[:, :, :, first : first + tile + MARG]
        picked = lax.dot_general(
            window_part, onehot, (((3,), (2,)), ((), ())), preferred_element_type=jnp.bfloat16
        )
        total = jnp.zeros(picked.shape[:3] + (tile,), jnp.float32)
        for tap_index in range(taps):
            total = total + picked[:, :, :, tap_index].astype(jnp.float32) * tap_weights[tap_index][None, :, None, None]
        pieces.append(total)
    return jnp.concatenate(pieces, axis=3)


CHUNKS = 2


def compress_block(echoes, range_phase, dev_count):
    _, channels, pulses, range_bins = echoes.shape
    second = range_bins // R1
    per_block = second // dev_count
    block = range_bins // dev_count
    cosine = jnp.cos(range_phase)
    sine = jnp.sin(range_phase)
    real_in = echoes[0].astype(jnp.float32)
    imag_in = echoes[1].astype(jnp.float32)
    spectrum = jnp.stack(
        [real_in * cosine - imag_in * sine, real_in * sine + imag_in * cosine]
    ).astype(jnp.bfloat16)
    spectrum = spectrum.reshape((2, channels, pulses, R1, second))
    section = apply_table(complex_table(R1, R1, R1, 1.0, 1.0), spectrum, 0, 3)
    twist_re, twist_im = phase_pair(R1, second, range_bins, 1.0, 1.0 / math.sqrt(range_bins))
    twist_re = twist_re[:, None, None, :]
    twist_im = twist_im[:, None, None, :]
    partial_terms = jnp.stack(
        [
            section[0] * twist_re - section[1] * twist_im,
            section[0] * twist_im + section[1] * twist_re,
        ]
    ).astype(jnp.bfloat16)
    partial_terms = partial_terms.transpose(0, 2, 3, 1, 4)
    second_table = complex_table(second, second, second, 1.0, 1.0).transpose(1, 0, 2, 3)
    second_table = second_table.reshape((dev_count, per_block, 2, 2, second))
    result = lax.dot_general(
        second_table, partial_terms, (((3, 4), (0, 4)), ((), ())), preferred_element_type=jnp.float32
    ).astype(jnp.bfloat16)
    return result.transpose(0, 2, 3, 4, 1, 5).reshape((dev_count, 2, channels, pulses, block))


def body(echoes, range_phase, offsets, tap_weights, channel_mix, azimuth_filter):
    dev_count = lax.axis_size("dev")
    _, channels, pulses, range_bins = echoes.shape
    block = range_bins // dev_count
    group_pulses = dev_count * pulses
    wide = group_pulses + group_pulses // 2
    forward = complex_table(wide, wide, wide, -1.0, 1.0 / math.sqrt(wide))
    own_table = forward[:, :, :, :group_pulses].reshape((2, wide, 2, dev_count, pulses))
    next_table = forward[:, :, :, group_pulses:].reshape((2, wide, 2, dev_count // 2, pulses))
    dims = (((2, 3, 4), (1, 0, 3)), ((), ()))
    step = channels // CHUNKS
    pieces = []
    for chunk in range(CHUNKS):
        result = compress_block(
            echoes[:, chunk * step : (chunk + 1) * step], range_phase, dev_count
        )
        turned = lax.all_to_all(result, "dev", 0, 0, tiled=True)
        following = shifted(turned[: dev_count // 2], "blk", -1)
        spectra = (
            lax.dot_general(own_table, turned, dims, preferred_element_type=jnp.float32)
            + lax.dot_general(next_table, following, dims, preferred_element_type=jnp.float32)
        ).astype(jnp.bfloat16)
        border = shifted(spectra[:, :, :, :MARG], "dev", -1)
        extended = jnp.concatenate([spectra, border], axis=3)
        pieces.append(migrate(extended, offsets, tap_weights, block))
    moved = jnp.concatenate(pieces, axis=2)
    mix_real = (
        azimuth_filter[0][:, None, :] * channel_mix[0]
        - azimuth_filter[1][:, None, :] * channel_mix[1]
    )
    mix_imag = (
        azimuth_filter[0][:, None, :] * channel_mix[1]
        + azimuth_filter[1][:, None, :] * channel_mix[0]
    )
    rows_real = []
    rows_imag = []
    for channel in range(channels):
        sum_real = jnp.zeros((wide, block), jnp.float32)
        sum_imag = jnp.zeros((wide, block), jnp.float32)
        for other_chan in range(channels):
            coef_real = mix_real[channel, other_chan][:, None]
            coef_imag = mix_imag[channel, other_chan][:, None]
            sum_real = (
                sum_real + coef_real * moved[0, :, other_chan] - coef_imag * moved[1, :, other_chan]
            )
            sum_imag = (
                sum_imag + coef_real * moved[1, :, other_chan] + coef_imag * moved[0, :, other_chan]
            )
        rows_real.append(sum_real)
        rows_imag.append(sum_imag)
    focused = jnp.stack([jnp.stack(rows_real, axis=1), jnp.stack(rows_imag, axis=1)]).astype(
        jnp.bfloat16
    )
    backward = complex_table(group_pulses, wide, wide, 1.0, 1.0 / math.sqrt(wide))
    image = apply_table(backward, focused, 0, 1).astype(jnp.bfloat16)
    return image.transpose(0, 2, 1, 3)


def solution(mesh):
    in_specs = (P(None, None, ("blk", "dev"), None), P(), P("dev"), P(), P(), P())
    out_specs = P(None, None, "blk", "dev")
    return jax.shard_map(body, mesh=mesh, in_specs=in_specs, out_specs=out_specs, check_vma=False)
```

```python
import math

import jax
import jax.numpy as jnp
from jax import lax
from jax.sharding import PartitionSpec as P


R1 = 128
MARG = 64


def shifted(block, axis, distance):
    devices = range(lax.axis_size(axis))
    route = [(i - distance, i) for i in devices if i - distance in devices]
    return lax.ppermute(block, axis, route)


def phase_pair(row_count, col_count, length, direction, factor):
    product = (
        jnp.arange(row_count, dtype=jnp.int32)[:, None]
        * jnp.arange(col_count, dtype=jnp.int32)[None, :]
        % length
    )
    angle = product.astype(jnp.float32) * (direction * 2.0 * math.pi / length)
    return (jnp.cos(angle) * factor, jnp.sin(angle) * factor)


def complex_table(row_count, col_count, length, direction, factor):
    cosine, sine = phase_pair(row_count, col_count, length, direction, factor)
    upper = jnp.stack([cosine, -sine], axis=1)
    lower = jnp.stack([sine, cosine], axis=1)
    return jnp.stack([upper, lower]).astype(jnp.bfloat16)


def apply_table(table, data, part_dim, index_dim):
    return lax.dot_general(
        table, data, (((2, 3), (part_dim, index_dim)), ((), ())), preferred_element_type=jnp.float32
    )


def migrate(extended, offsets, tap_weights, block):
    tile = min(128, block)
    taps = tap_weights.shape[0]
    pieces = []
    for tile_index in range(block // tile):
        first = tile_index * tile
        rows_here = jnp.arange(tile, dtype=jnp.int32)
        target = rows_here + offsets[first : first + tile]
        columns = jnp.arange(tile + MARG, dtype=jnp.int32)
        tap_range = jnp.arange(taps, dtype=jnp.int32)
        onehot = (
            columns[None, None, :] == target[None, :, None] + tap_range[:, None, None]
        ).astype(jnp.bfloat16)
        window_part = extended[:, :, :, first : first + tile + MARG]
        picked = lax.dot_general(
            window_part, onehot, (((3,), (2,)), ((), ())), preferred_element_type=jnp.bfloat16
        )
        total = jnp.zeros(picked.shape[:3] + (tile,), jnp.float32)
        for tap_index in range(taps):
            total = total + picked[:, :, :, tap_index].astype(jnp.float32) * tap_weights[tap_index][None, :, None, None]
        pieces.append(total)
    return jnp.concatenate(pieces, axis=3)


SPLIT = (3, 1)


def compress_block(echoes, range_phase, dev_count):
    _, channels, pulses, range_bins = echoes.shape
    second = range_bins // R1
    per_block = second // dev_count
    block = range_bins // dev_count
    cosine = jnp.cos(range_phase)
    sine = jnp.sin(range_phase)
    real_in = echoes[0].astype(jnp.float32)
    imag_in = echoes[1].astype(jnp.float32)
    spectrum = jnp.stack(
        [real_in * cosine - imag_in * sine, real_in * sine + imag_in * cosine]
    ).astype(jnp.bfloat16)
    spectrum = spectrum.reshape((2, channels, pulses, R1, second))
    section = apply_table(complex_table(R1, R1, R1, 1.0, 1.0), spectrum, 0, 3)
    twist_re, twist_im = phase_pair(R1, second, range_bins, 1.0, 1.0 / math.sqrt(range_bins))
    twist_re = twist_re[:, None, None, :]
    twist_im = twist_im[:, None, None, :]
    partial_terms = jnp.stack(
        [
            section[0] * twist_re - section[1] * twist_im,
            section[0] * twist_im + section[1] * twist_re,
        ]
    ).astype(jnp.bfloat16)
    partial_terms = partial_terms.transpose(0, 2, 3, 1, 4)
    second_table = complex_table(second, second, second, 1.0, 1.0).transpose(1, 0, 2, 3)
    second_table = second_table.reshape((dev_count, per_block, 2, 2, second))
    result = lax.dot_general(
        second_table, partial_terms, (((3, 4), (0, 4)), ((), ())), preferred_element_type=jnp.float32
    ).astype(jnp.bfloat16)
    return result.transpose(0, 2, 3, 4, 1, 5).reshape((dev_count, 2, channels, pulses, block))


def body(echoes, range_phase, offsets, tap_weights, channel_mix, azimuth_filter):
    dev_count = lax.axis_size("dev")
    _, _, pulses, range_bins = echoes.shape
    block = range_bins // dev_count
    group_pulses = dev_count * pulses
    wide = group_pulses + group_pulses // 2
    forward = complex_table(wide, wide, wide, -1.0, 1.0 / math.sqrt(wide))
    own_table = forward[:, :, :, :group_pulses].reshape((2, wide, 2, dev_count, pulses))
    next_table = forward[:, :, :, group_pulses:].reshape((2, wide, 2, dev_count // 2, pulses))
    dims = (((2, 3, 4), (1, 0, 3)), ((), ()))
    pieces = []
    first = 0
    for width in SPLIT:
        result = compress_block(echoes[:, first : first + width], range_phase, dev_count)
        first += width
        turned = lax.all_to_all(result, "dev", 0, 0, tiled=True)
        following = shifted(turned[: dev_count // 2], "blk", -1)
        spectra = (
            lax.dot_general(own_table, turned, dims, preferred_element_type=jnp.float32)
            + lax.dot_general(next_table, following, dims, preferred_element_type=jnp.float32)
        ).astype(jnp.bfloat16)
        border = shifted(spectra[:, :, :, :MARG], "dev", -1)
        extended = jnp.concatenate([spectra, border], axis=3)
        pieces.append(migrate(extended, offsets, tap_weights, block))
    moved = jnp.concatenate(pieces, axis=2)
    mix_real = (
        azimuth_filter[0][:, None, :] * channel_mix[0]
        - azimuth_filter[1][:, None, :] * channel_mix[1]
    )
    mix_imag = (
        azimuth_filter[0][:, None, :] * channel_mix[1]
        + azimuth_filter[1][:, None, :] * channel_mix[0]
    )
    mix_real = mix_real.transpose(2, 0, 1)[:, :, :, None]
    mix_imag = mix_imag.transpose(2, 0, 1)[:, :, :, None]
    moved_real = moved[0][:, None]
    moved_imag = moved[1][:, None]
    focused = jnp.stack(
        [
            (mix_real * moved_real - mix_imag * moved_imag).sum(axis=2),
            (mix_real * moved_imag + mix_imag * moved_real).sum(axis=2),
        ]
    ).astype(jnp.bfloat16)
    backward = complex_table(group_pulses, wide, wide, 1.0, 1.0 / math.sqrt(wide))
    image = apply_table(backward, focused, 0, 1).astype(jnp.bfloat16)
    return image.transpose(0, 2, 1, 3)


def solution(mesh):
    in_specs = (P(None, None, ("blk", "dev"), None), P(), P("dev"), P(), P(), P())
    out_specs = P(None, None, "blk", "dev")
    return jax.shard_map(body, mesh=mesh, in_specs=in_specs, out_specs=out_specs, check_vma=False)
```

```python
import math

import jax
import jax.numpy as jnp
from jax import lax
from jax.sharding import PartitionSpec as P


R1 = 128
MARG = 64


def shifted(block, axis, distance):
    devices = range(lax.axis_size(axis))
    route = [(i - distance, i) for i in devices if i - distance in devices]
    return lax.ppermute(block, axis, route)


def phase_pair(row_count, col_count, length, direction, factor):
    product = (
        jnp.arange(row_count, dtype=jnp.int32)[:, None]
        * jnp.arange(col_count, dtype=jnp.int32)[None, :]
        % length
    )
    angle = product.astype(jnp.float32) * (direction * 2.0 * math.pi / length)
    return (jnp.cos(angle) * factor, jnp.sin(angle) * factor)


def complex_table(row_count, col_count, length, direction, factor):
    cosine, sine = phase_pair(row_count, col_count, length, direction, factor)
    upper = jnp.stack([cosine, -sine], axis=1)
    lower = jnp.stack([sine, cosine], axis=1)
    return jnp.stack([upper, lower]).astype(jnp.bfloat16)


def apply_table(table, data, part_dim, index_dim):
    return lax.dot_general(
        table, data, (((2, 3), (part_dim, index_dim)), ((), ())), preferred_element_type=jnp.float32
    )


def migrate(spectra, border, offsets, tap_weights, block):
    tile = min(128, block)
    taps = tap_weights.shape[0]
    pieces = []
    for tile_index in range(block // tile):
        first = tile_index * tile
        rows_here = jnp.arange(tile, dtype=jnp.int32)
        target = rows_here + offsets[first : first + tile]
        columns = jnp.arange(tile + MARG, dtype=jnp.int32)
        tap_range = jnp.arange(taps, dtype=jnp.int32)
        onehot = (
            columns[None, None, :] == target[None, :, None] + tap_range[:, None, None]
        ).astype(jnp.bfloat16)
        if first + tile + MARG <= block:
            window_part = spectra[:, :, :, first : first + tile + MARG]
        else:
            window_part = jnp.concatenate([spectra[:, :, :, first:], border], axis=3)
        picked = lax.dot_general(
            window_part, onehot, (((3,), (2,)), ((), ())), preferred_element_type=jnp.bfloat16
        )
        total = jnp.zeros(picked.shape[:3] + (tile,), jnp.float32)
        for tap_index in range(taps):
            total = total + picked[:, :, :, tap_index].astype(jnp.float32) * tap_weights[
                tap_index
            ][None, :, None, None]
        pieces.append(total)
    return jnp.concatenate(pieces, axis=3)


CHUNKS = 2


def compress_block(echoes, range_phase, dev_count):
    _, channels, pulses, range_bins = echoes.shape
    second = range_bins // R1
    per_block = second // dev_count
    block = range_bins // dev_count
    cosine = jnp.cos(range_phase)
    sine = jnp.sin(range_phase)
    real_in = echoes[0].astype(jnp.float32)
    imag_in = echoes[1].astype(jnp.float32)
    spectrum = jnp.stack(
        [real_in * cosine - imag_in * sine, real_in * sine + imag_in * cosine]
    ).astype(jnp.bfloat16)
    spectrum = spectrum.reshape((2, channels, pulses, R1, second))
    section = apply_table(complex_table(R1, R1, R1, 1.0, 1.0), spectrum, 0, 3)
    twist_re, twist_im = phase_pair(R1, second, range_bins, 1.0, 1.0 / math.sqrt(range_bins))
    twist_re = twist_re[:, None, None, :]
    twist_im = twist_im[:, None, None, :]
    partial_terms = jnp.stack(
        [
            section[0] * twist_re - section[1] * twist_im,
            section[0] * twist_im + section[1] * twist_re,
        ]
    ).astype(jnp.bfloat16)
    partial_terms = partial_terms.transpose(0, 2, 3, 1, 4)
    second_table = complex_table(second, second, second, 1.0, 1.0).transpose(1, 0, 2, 3)
    second_table = second_table.reshape((dev_count, per_block, 2, 2, second))
    result = lax.dot_general(
        second_table, partial_terms, (((3, 4), (0, 4)), ((), ())), preferred_element_type=jnp.float32
    ).astype(jnp.bfloat16)
    return result.transpose(0, 2, 3, 4, 1, 5).reshape((dev_count, 2, channels, pulses, block))


def body(echoes, range_phase, offsets, tap_weights, channel_mix, azimuth_filter):
    dev_count = lax.axis_size("dev")
    _, channels, pulses, range_bins = echoes.shape
    block = range_bins // dev_count
    group_pulses = dev_count * pulses
    wide = group_pulses + group_pulses // 2
    forward = complex_table(wide, wide, wide, -1.0, 1.0 / math.sqrt(wide))
    own_table = forward[:, :, :, :group_pulses].reshape((2, wide, 2, dev_count, pulses))
    next_table = forward[:, :, :, group_pulses:].reshape((2, wide, 2, dev_count // 2, pulses))
    dims = (((2, 3, 4), (1, 0, 3)), ((), ()))
    step = channels // CHUNKS
    pieces = []
    for chunk in range(CHUNKS):
        result = compress_block(
            echoes[:, chunk * step : (chunk + 1) * step], range_phase, dev_count
        )
        turned = lax.all_to_all(result, "dev", 0, 0, tiled=True)
        following = shifted(turned[: dev_count // 2], "blk", -1)
        spectra = (
            lax.dot_general(own_table, turned, dims, preferred_element_type=jnp.float32)
            + lax.dot_general(next_table, following, dims, preferred_element_type=jnp.float32)
        ).astype(jnp.bfloat16)
        border = shifted(spectra[:, :, :, :MARG], "dev", -1)
        pieces.append(migrate(spectra, border, offsets, tap_weights, block))
    moved = jnp.concatenate(pieces, axis=2)
    mix_real = (
        azimuth_filter[0][:, None, :] * channel_mix[0]
        - azimuth_filter[1][:, None, :] * channel_mix[1]
    )
    mix_imag = (
        azimuth_filter[0][:, None, :] * channel_mix[1]
        + azimuth_filter[1][:, None, :] * channel_mix[0]
    )
    rows_real = []
    rows_imag = []
    for channel in range(channels):
        sum_real = jnp.zeros((wide, block), jnp.float32)
        sum_imag = jnp.zeros((wide, block), jnp.float32)
        for other_chan in range(channels):
            coef_real = mix_real[channel, other_chan][:, None]
            coef_imag = mix_imag[channel, other_chan][:, None]
            sum_real = (
                sum_real + coef_real * moved[0, :, other_chan] - coef_imag * moved[1, :, other_chan]
            )
            sum_imag = (
                sum_imag + coef_real * moved[1, :, other_chan] + coef_imag * moved[0, :, other_chan]
            )
        rows_real.append(sum_real)
        rows_imag.append(sum_imag)
    focused = jnp.stack([jnp.stack(rows_real, axis=1), jnp.stack(rows_imag, axis=1)]).astype(
        jnp.bfloat16
    )
    backward = complex_table(group_pulses, wide, wide, 1.0, 1.0 / math.sqrt(wide))
    image = apply_table(backward, focused, 0, 1).astype(jnp.bfloat16)
    return image.transpose(0, 2, 1, 3)


def solution(mesh):
    in_specs = (P(None, None, ("blk", "dev"), None), P(), P("dev"), P(), P(), P())
    out_specs = P(None, None, "blk", "dev")
    return jax.shard_map(body, mesh=mesh, in_specs=in_specs, out_specs=out_specs, check_vma=False)
```

```python
import math

import jax
import jax.numpy as jnp
from jax import lax
from jax.experimental import pallas as pl
from jax.experimental.pallas import tpu as pltpu
from jax.sharding import PartitionSpec as P


R1 = 128
MARG = 64


def shifted(block, axis, distance):
    devices = range(lax.axis_size(axis))
    route = [(i - distance, i) for i in devices if i - distance in devices]
    return lax.ppermute(block, axis, route)


def phase_pair(row_count, col_count, length, direction, factor):
    product = (
        jnp.arange(row_count, dtype=jnp.int32)[:, None]
        * jnp.arange(col_count, dtype=jnp.int32)[None, :]
        % length
    )
    angle = product.astype(jnp.float32) * (direction * 2.0 * math.pi / length)
    return (jnp.cos(angle) * factor, jnp.sin(angle) * factor)


def complex_table(row_count, col_count, length, direction, factor):
    cosine, sine = phase_pair(row_count, col_count, length, direction, factor)
    upper = jnp.stack([cosine, -sine], axis=1)
    lower = jnp.stack([sine, cosine], axis=1)
    return jnp.stack([upper, lower]).astype(jnp.bfloat16)


def apply_table(table, data, part_dim, index_dim):
    return lax.dot_general(
        table, data, (((2, 3), (part_dim, index_dim)), ((), ())), preferred_element_type=jnp.float32
    )


def compress(echoes, range_phase):
    cosine = jnp.cos(range_phase)
    sine = jnp.sin(range_phase)
    real_in = echoes[0].astype(jnp.float32)
    imag_in = echoes[1].astype(jnp.float32)
    spectrum = jnp.stack(
        [real_in * cosine - imag_in * sine, real_in * sine + imag_in * cosine]
    ).astype(jnp.bfloat16)
    channels = spectrum.shape[1]
    pulses = spectrum.shape[2]
    range_bins = spectrum.shape[3]
    second = range_bins // R1
    spectrum = spectrum.reshape((2, channels, pulses, R1, second))
    section = apply_table(complex_table(R1, R1, R1, 1.0, 1.0), spectrum, 0, 3)
    twist_re, twist_im = phase_pair(R1, second, range_bins, 1.0, 1.0 / math.sqrt(range_bins))
    twist_re = twist_re[:, None, None, :]
    twist_im = twist_im[:, None, None, :]
    partial_terms = jnp.stack(
        [
            section[0] * twist_re - section[1] * twist_im,
            section[0] * twist_im + section[1] * twist_re,
        ]
    ).astype(jnp.bfloat16)
    result = apply_table(
        complex_table(second, second, second, 1.0, 1.0), partial_terms, 0, 4
    ).astype(jnp.bfloat16)
    return result.transpose(0, 3, 4, 1, 2).reshape((2, channels, pulses, range_bins))


def doppler(window):
    wide = window.shape[2]
    forward = complex_table(wide, wide, wide, -1.0, 1.0 / math.sqrt(wide))
    return apply_table(forward, window, 0, 2).astype(jnp.bfloat16)


LANE = 128


def migrate_mix_kernel(spec_ref, *refs):
    *extra, onehot_ref, taps_ref, mr_ref, mi_ref, out_ref = refs
    parts, chans, wide, width = spec_ref.shape
    taps = taps_ref.shape[0]
    for t in range(out_ref.shape[3] // LANE):
        moved = {}
        for p in range(parts):
            for d in range(chans):
                lead = spec_ref[p, d, :, t * LANE : (t + 1) * LANE]
                if (t + 2) * LANE <= width:
                    tail = spec_ref[p, d, :, (t + 1) * LANE : (t + 2) * LANE]
                else:
                    tail = extra[0][p, d]
                picked = jnp.dot(
                    lead, onehot_ref[t, :LANE, :], preferred_element_type=jnp.float32
                ) + jnp.dot(tail, onehot_ref[t, LANE:, :], preferred_element_type=jnp.float32)
                total = picked[:, :LANE] * taps_ref[0]
                for j in range(1, taps):
                    total = total + picked[:, j * LANE : (j + 1) * LANE] * taps_ref[j]
                moved[p, d] = total
        for c in range(chans):
            real = mr_ref[c, 0] * moved[0, 0] - mi_ref[c, 0] * moved[1, 0]
            imag = mr_ref[c, 0] * moved[1, 0] + mi_ref[c, 0] * moved[0, 0]
            for d in range(1, chans):
                real = real + mr_ref[c, d] * moved[0, d] - mi_ref[c, d] * moved[1, d]
                imag = imag + mr_ref[c, d] * moved[1, d] + mi_ref[c, d] * moved[0, d]
            out_ref[0, c, :, t * LANE : (t + 1) * LANE] = real.astype(out_ref.dtype)
            out_ref[1, c, :, t * LANE : (t + 1) * LANE] = imag.astype(out_ref.dtype)


def migrate_mix(spectra, extra, onehot, taps_b, mr_b, mi_b, tiles):
    parts, chans, wide, _ = spectra.shape
    vmem = pl.BlockSpec(memory_space=pltpu.VMEM)
    operands = (spectra, *extra, onehot, taps_b, mr_b, mi_b)
    return pl.pallas_call(
        migrate_mix_kernel,
        out_shape=jax.ShapeDtypeStruct((parts, chans, wide, tiles * LANE), jnp.bfloat16),
        in_specs=[vmem] * len(operands),
        out_specs=vmem,
    )(*operands)


CHUNKS = 1


def compress_block(echoes, range_phase, dev_count):
    parts, channels, pulses, range_bins = echoes.shape
    second = range_bins // R1
    per_block = second // dev_count
    block = range_bins // dev_count
    cosine = jnp.cos(range_phase)
    sine = jnp.sin(range_phase)
    real_in = echoes[0].astype(jnp.float32)
    imag_in = echoes[1].astype(jnp.float32)
    spectrum = jnp.stack(
        [real_in * cosine - imag_in * sine, real_in * sine + imag_in * cosine]
    ).astype(jnp.bfloat16)
    spectrum = spectrum.reshape((2, channels, pulses, R1, second))
    section = apply_table(complex_table(R1, R1, R1, 1.0, 1.0), spectrum, 0, 3)
    twist_re, twist_im = phase_pair(R1, second, range_bins, 1.0, 1.0 / math.sqrt(range_bins))
    twist_re = twist_re[:, None, None, :]
    twist_im = twist_im[:, None, None, :]
    partial_terms = jnp.stack(
        [
            section[0] * twist_re - section[1] * twist_im,
            section[0] * twist_im + section[1] * twist_re,
        ]
    ).astype(jnp.bfloat16)
    partial_terms = partial_terms.transpose(0, 2, 3, 1, 4)
    second_table = complex_table(second, second, second, 1.0, 1.0).transpose(1, 0, 2, 3)
    second_table = second_table.reshape((dev_count, per_block, 2, 2, second))
    result = lax.dot_general(
        second_table, partial_terms, (((3, 4), (0, 4)), ((), ())), preferred_element_type=jnp.float32
    ).astype(jnp.bfloat16)
    return result.transpose(0, 2, 3, 4, 1, 5).reshape((dev_count, 2, channels, pulses, block))


def body(echoes, range_phase, offsets, tap_weights, channel_mix, azimuth_filter):
    dev_count = lax.axis_size("dev")
    parts, channels, pulses, range_bins = echoes.shape
    block = range_bins // dev_count
    group_pulses = dev_count * pulses
    wide = group_pulses + group_pulses // 2
    forward = complex_table(wide, wide, wide, -1.0, 1.0 / math.sqrt(wide))
    own_table = forward[:, :, :, :group_pulses].reshape((2, wide, 2, dev_count, pulses))
    next_table = forward[:, :, :, group_pulses:].reshape((2, wide, 2, dev_count // 2, pulses))
    dims = (((2, 3, 4), (1, 0, 3)), ((), ()))
    step = channels // CHUNKS
    pieces = []
    for chunk in range(CHUNKS):
        with jax.named_scope(f"c{chunk}"):
            result = compress_block(
                echoes[:, chunk * step : (chunk + 1) * step], range_phase, dev_count
            )
        with jax.named_scope(f"x{chunk}"):
            turned = lax.all_to_all(result, "dev", 0, 0, tiled=True)
        with jax.named_scope(f"p{chunk}"):
            following = shifted(turned[: dev_count // 2], "blk", -1)
            spectra = (
                lax.dot_general(own_table, turned, dims, preferred_element_type=jnp.float32)
                + lax.dot_general(next_table, following, dims, preferred_element_type=jnp.float32)
            ).astype(jnp.bfloat16)
            pieces.append(spectra.transpose(0, 2, 1, 3))
    spectra = jnp.concatenate(pieces, axis=1)
    mix_real = (
        azimuth_filter[0][:, None, :] * channel_mix[0]
        - azimuth_filter[1][:, None, :] * channel_mix[1]
    )
    mix_imag = (
        azimuth_filter[0][:, None, :] * channel_mix[1]
        + azimuth_filter[1][:, None, :] * channel_mix[0]
    )
    taps = tap_weights.shape[0]
    tiles = block // LANE
    rows = jnp.arange(LANE, dtype=jnp.int32)
    span = jnp.arange(2 * LANE, dtype=jnp.int32)
    tap_range = jnp.arange(taps, dtype=jnp.int32)
    target = rows[None, :] + offsets.astype(jnp.int32).reshape(tiles, LANE)
    onehot = (
        span[None, :, None, None] == target[:, None, None, :] + tap_range[None, None, :, None]
    ).astype(jnp.bfloat16).reshape(tiles, 2 * LANE, taps * LANE)
    taps_b = jnp.broadcast_to(tap_weights[:, :, None], (taps, wide, LANE))
    mr_b = jnp.broadcast_to(mix_real[:, :, :, None], (channels, channels, wide, LANE))
    mi_b = jnp.broadcast_to(mix_imag[:, :, :, None], (channels, channels, wide, LANE))
    border = shifted(spectra[:, :, :, :LANE], "dev", -1)
    head = migrate_mix(spectra, (), onehot, taps_b, mr_b, mi_b, tiles - 1)
    last = migrate_mix(
        spectra[:, :, :, block - LANE :], (border,), onehot[tiles - 1 :], taps_b, mr_b, mi_b, 1
    )
    focused = jnp.concatenate([head, last], axis=3)
    backward = complex_table(group_pulses, wide, wide, 1.0, 1.0 / math.sqrt(wide))
    image = apply_table(backward, focused, 0, 2).astype(jnp.bfloat16)
    return image.transpose(0, 2, 1, 3)


def solution(mesh):
    in_specs = (P(None, None, ("blk", "dev"), None), P(), P("dev"), P(), P(), P())
    out_specs = P(None, None, "blk", "dev")
    return jax.shard_map(body, mesh=mesh, in_specs=in_specs, out_specs=out_specs, check_vma=False)
```

```python
import math

import jax
import jax.numpy as jnp
from jax import lax
from jax.experimental import pallas as pl
from jax.experimental.pallas import tpu as pltpu
from jax.sharding import PartitionSpec as P


R1 = 128
MARG = 64


def shifted(block, axis, distance):
    devices = range(lax.axis_size(axis))
    route = [(i - distance, i) for i in devices if i - distance in devices]
    return lax.ppermute(block, axis, route)


def phase_pair(row_count, col_count, length, direction, factor):
    product = (
        jnp.arange(row_count, dtype=jnp.int32)[:, None]
        * jnp.arange(col_count, dtype=jnp.int32)[None, :]
        % length
    )
    angle = product.astype(jnp.float32) * (direction * 2.0 * math.pi / length)
    return (jnp.cos(angle) * factor, jnp.sin(angle) * factor)


def complex_table(row_count, col_count, length, direction, factor):
    cosine, sine = phase_pair(row_count, col_count, length, direction, factor)
    upper = jnp.stack([cosine, -sine], axis=1)
    lower = jnp.stack([sine, cosine], axis=1)
    return jnp.stack([upper, lower]).astype(jnp.bfloat16)


def apply_table(table, data, part_dim, index_dim):
    return lax.dot_general(
        table, data, (((2, 3), (part_dim, index_dim)), ((), ())), preferred_element_type=jnp.float32
    )


def compress(echoes, range_phase):
    cosine = jnp.cos(range_phase)
    sine = jnp.sin(range_phase)
    real_in = echoes[0].astype(jnp.float32)
    imag_in = echoes[1].astype(jnp.float32)
    spectrum = jnp.stack(
        [real_in * cosine - imag_in * sine, real_in * sine + imag_in * cosine]
    ).astype(jnp.bfloat16)
    channels = spectrum.shape[1]
    pulses = spectrum.shape[2]
    range_bins = spectrum.shape[3]
    second = range_bins // R1
    spectrum = spectrum.reshape((2, channels, pulses, R1, second))
    section = apply_table(complex_table(R1, R1, R1, 1.0, 1.0), spectrum, 0, 3)
    twist_re, twist_im = phase_pair(R1, second, range_bins, 1.0, 1.0 / math.sqrt(range_bins))
    twist_re = twist_re[:, None, None, :]
    twist_im = twist_im[:, None, None, :]
    partial_terms = jnp.stack(
        [
            section[0] * twist_re - section[1] * twist_im,
            section[0] * twist_im + section[1] * twist_re,
        ]
    ).astype(jnp.bfloat16)
    result = apply_table(
        complex_table(second, second, second, 1.0, 1.0), partial_terms, 0, 4
    ).astype(jnp.bfloat16)
    return result.transpose(0, 3, 4, 1, 2).reshape((2, channels, pulses, range_bins))


def doppler(window):
    wide = window.shape[2]
    forward = complex_table(wide, wide, wide, -1.0, 1.0 / math.sqrt(wide))
    return apply_table(forward, window, 0, 2).astype(jnp.bfloat16)


LANE = 128


def migrate_mix_kernel(lead_ref, tail_ref, onehot_ref, taps_ref, mr_ref, mi_ref, out_ref):
    parts, chans = lead_ref.shape[:2]
    taps = taps_ref.shape[0]
    moved = {}
    for p in range(parts):
        for d in range(chans):
            picked = jnp.dot(
                lead_ref[p, d], onehot_ref[0, :LANE, :], preferred_element_type=jnp.float32
            ) + jnp.dot(tail_ref[p, d], onehot_ref[0, LANE:, :], preferred_element_type=jnp.float32)
            total = picked[:, :LANE] * taps_ref[0]
            for j in range(1, taps):
                total = total + picked[:, j * LANE : (j + 1) * LANE] * taps_ref[j]
            moved[p, d] = total
    for c in range(chans):
        real = mr_ref[c, 0] * moved[0, 0] - mi_ref[c, 0] * moved[1, 0]
        imag = mr_ref[c, 0] * moved[1, 0] + mi_ref[c, 0] * moved[0, 0]
        for d in range(1, chans):
            real = real + mr_ref[c, d] * moved[0, d] - mi_ref[c, d] * moved[1, d]
            imag = imag + mr_ref[c, d] * moved[1, d] + mi_ref[c, d] * moved[0, d]
        out_ref[0, c] = real.astype(out_ref.dtype)
        out_ref[1, c] = imag.astype(out_ref.dtype)


def migrate_mix(spectra, tail, onehot, taps_c, mr_c, mi_c, tiles, tail_shift):
    parts, chans, wide, _ = spectra.shape
    rows = min(LANE, wide)
    taps = taps_c.shape[0]
    block = (parts, chans, rows, LANE)
    return pl.pallas_call(
        migrate_mix_kernel,
        out_shape=jax.ShapeDtypeStruct((parts, chans, wide, tiles * LANE), jnp.bfloat16),
        grid=(tiles, wide // rows),
        in_specs=[
            pl.BlockSpec(block, lambda t, f: (0, 0, f, t)),
            pl.BlockSpec(block, lambda t, f: (0, 0, f, t + tail_shift)),
            pl.BlockSpec((1, 2 * LANE, taps * LANE), lambda t, f: (t, 0, 0)),
            pl.BlockSpec((taps, rows, 1), lambda t, f: (0, f, 0)),
            pl.BlockSpec((chans, chans, rows, 1), lambda t, f: (0, 0, f, 0)),
            pl.BlockSpec((chans, chans, rows, 1), lambda t, f: (0, 0, f, 0)),
        ],
        out_specs=pl.BlockSpec(block, lambda t, f: (0, 0, f, t)),
    )(spectra, tail, onehot, taps_c, mr_c, mi_c)


CHUNKS = 1


def compress_block(echoes, range_phase, dev_count):
    parts, channels, pulses, range_bins = echoes.shape
    second = range_bins // R1
    per_block = second // dev_count
    block = range_bins // dev_count
    cosine = jnp.cos(range_phase)
    sine = jnp.sin(range_phase)
    real_in = echoes[0].astype(jnp.float32)
    imag_in = echoes[1].astype(jnp.float32)
    spectrum = jnp.stack(
        [real_in * cosine - imag_in * sine, real_in * sine + imag_in * cosine]
    ).astype(jnp.bfloat16)
    spectrum = spectrum.reshape((2, channels, pulses, R1, second))
    section = apply_table(complex_table(R1, R1, R1, 1.0, 1.0), spectrum, 0, 3)
    twist_re, twist_im = phase_pair(R1, second, range_bins, 1.0, 1.0 / math.sqrt(range_bins))
    twist_re = twist_re[:, None, None, :]
    twist_im = twist_im[:, None, None, :]
    partial_terms = jnp.stack(
        [
            section[0] * twist_re - section[1] * twist_im,
            section[0] * twist_im + section[1] * twist_re,
        ]
    ).astype(jnp.bfloat16)
    partial_terms = partial_terms.transpose(0, 2, 3, 1, 4)
    second_table = complex_table(second, second, second, 1.0, 1.0).transpose(1, 0, 2, 3)
    second_table = second_table.reshape((dev_count, per_block, 2, 2, second))
    result = lax.dot_general(
        second_table, partial_terms, (((3, 4), (0, 4)), ((), ())), preferred_element_type=jnp.float32
    ).astype(jnp.bfloat16)
    return result.transpose(0, 2, 3, 4, 1, 5).reshape((dev_count, 2, channels, pulses, block))


def body(echoes, range_phase, offsets, tap_weights, channel_mix, azimuth_filter):
    dev_count = lax.axis_size("dev")
    parts, channels, pulses, range_bins = echoes.shape
    block = range_bins // dev_count
    group_pulses = dev_count * pulses
    wide = group_pulses + group_pulses // 2
    forward = complex_table(wide, wide, wide, -1.0, 1.0 / math.sqrt(wide))
    own_table = forward[:, :, :, :group_pulses].reshape((2, wide, 2, dev_count, pulses))
    next_table = forward[:, :, :, group_pulses:].reshape((2, wide, 2, dev_count // 2, pulses))
    dims = (((2, 3, 4), (1, 0, 3)), ((), ()))
    step = channels // CHUNKS
    pieces = []
    for chunk in range(CHUNKS):
        with jax.named_scope(f"c{chunk}"):
            result = compress_block(
                echoes[:, chunk * step : (chunk + 1) * step], range_phase, dev_count
            )
        with jax.named_scope(f"x{chunk}"):
            turned = lax.all_to_all(result, "dev", 0, 0, tiled=True)
        with jax.named_scope(f"p{chunk}"):
            following = shifted(turned[: dev_count // 2], "blk", -1)
            spectra = (
                lax.dot_general(own_table, turned, dims, preferred_element_type=jnp.float32)
                + lax.dot_general(next_table, following, dims, preferred_element_type=jnp.float32)
            ).astype(jnp.bfloat16)
            pieces.append(spectra.transpose(0, 2, 1, 3))
    spectra = jnp.concatenate(pieces, axis=1)
    mix_real = (
        azimuth_filter[0][:, None, :] * channel_mix[0]
        - azimuth_filter[1][:, None, :] * channel_mix[1]
    )
    mix_imag = (
        azimuth_filter[0][:, None, :] * channel_mix[1]
        + azimuth_filter[1][:, None, :] * channel_mix[0]
    )
    taps = tap_weights.shape[0]
    tiles = block // LANE
    rows = jnp.arange(LANE, dtype=jnp.int32)
    span = jnp.arange(2 * LANE, dtype=jnp.int32)
    tap_range = jnp.arange(taps, dtype=jnp.int32)
    target = rows[None, :] + offsets.astype(jnp.int32).reshape(tiles, LANE)
    onehot = (
        span[None, :, None, None] == target[:, None, None, :] + tap_range[None, None, :, None]
    ).astype(jnp.bfloat16).reshape(tiles, 2 * LANE, taps * LANE)
    taps_c = tap_weights[:, :, None]
    mr_c = mix_real[:, :, :, None]
    mi_c = mix_imag[:, :, :, None]
    border = shifted(spectra[:, :, :, :LANE], "dev", -1)
    head = migrate_mix(spectra, spectra, onehot, taps_c, mr_c, mi_c, tiles - 1, 1)
    last = migrate_mix(
        spectra[:, :, :, block - LANE :], border, onehot[tiles - 1 :], taps_c, mr_c, mi_c, 1, 0
    )
    focused = jnp.concatenate([head, last], axis=3)
    backward = complex_table(group_pulses, wide, wide, 1.0, 1.0 / math.sqrt(wide))
    image = apply_table(backward, focused, 0, 2).astype(jnp.bfloat16)
    return image.transpose(0, 2, 1, 3)


def solution(mesh):
    in_specs = (P(None, None, ("blk", "dev"), None), P(), P("dev"), P(), P(), P())
    out_specs = P(None, None, "blk", "dev")
    return jax.shard_map(body, mesh=mesh, in_specs=in_specs, out_specs=out_specs, check_vma=False)
```

```python
import math

import jax
import jax.numpy as jnp
from jax import lax
from jax.experimental import pallas as pl
from jax.experimental.pallas import tpu as pltpu
from jax.sharding import PartitionSpec as P


R1 = 128
MARG = 64


def shifted(block, axis, distance):
    devices = range(lax.axis_size(axis))
    route = [(i - distance, i) for i in devices if i - distance in devices]
    return lax.ppermute(block, axis, route)


def phase_pair(row_count, col_count, length, direction, factor):
    product = (
        jnp.arange(row_count, dtype=jnp.int32)[:, None]
        * jnp.arange(col_count, dtype=jnp.int32)[None, :]
        % length
    )
    angle = product.astype(jnp.float32) * (direction * 2.0 * math.pi / length)
    return (jnp.cos(angle) * factor, jnp.sin(angle) * factor)


def complex_table(row_count, col_count, length, direction, factor):
    cosine, sine = phase_pair(row_count, col_count, length, direction, factor)
    upper = jnp.stack([cosine, -sine], axis=1)
    lower = jnp.stack([sine, cosine], axis=1)
    return jnp.stack([upper, lower]).astype(jnp.bfloat16)


def apply_table(table, data, part_dim, index_dim):
    return lax.dot_general(
        table, data, (((2, 3), (part_dim, index_dim)), ((), ())), preferred_element_type=jnp.float32
    )


def compress(echoes, range_phase):
    cosine = jnp.cos(range_phase)
    sine = jnp.sin(range_phase)
    real_in = echoes[0].astype(jnp.float32)
    imag_in = echoes[1].astype(jnp.float32)
    spectrum = jnp.stack(
        [real_in * cosine - imag_in * sine, real_in * sine + imag_in * cosine]
    ).astype(jnp.bfloat16)
    channels = spectrum.shape[1]
    pulses = spectrum.shape[2]
    range_bins = spectrum.shape[3]
    second = range_bins // R1
    spectrum = spectrum.reshape((2, channels, pulses, R1, second))
    section = apply_table(complex_table(R1, R1, R1, 1.0, 1.0), spectrum, 0, 3)
    twist_re, twist_im = phase_pair(R1, second, range_bins, 1.0, 1.0 / math.sqrt(range_bins))
    twist_re = twist_re[:, None, None, :]
    twist_im = twist_im[:, None, None, :]
    partial_terms = jnp.stack(
        [
            section[0] * twist_re - section[1] * twist_im,
            section[0] * twist_im + section[1] * twist_re,
        ]
    ).astype(jnp.bfloat16)
    result = apply_table(
        complex_table(second, second, second, 1.0, 1.0), partial_terms, 0, 4
    ).astype(jnp.bfloat16)
    return result.transpose(0, 3, 4, 1, 2).reshape((2, channels, pulses, range_bins))


def doppler(window):
    wide = window.shape[2]
    forward = complex_table(wide, wide, wide, -1.0, 1.0 / math.sqrt(wide))
    return apply_table(forward, window, 0, 2).astype(jnp.bfloat16)


LANE = 128


def migrate_mix_kernel(lead_ref, tail_ref, onehot_ref, taps_ref, mr_ref, mi_ref, out_ref):
    parts, chans, rows, _ = lead_ref.shape
    taps = taps_ref.shape[0]
    stack = parts * chans * rows
    window = jnp.concatenate(
        [lead_ref[...].reshape(stack, LANE), tail_ref[...].reshape(stack, LANE)], axis=1
    )
    picked = jnp.dot(window, onehot_ref[0], preferred_element_type=jnp.float32)
    total = picked[:, :LANE].reshape(parts * chans, rows, LANE) * taps_ref[0]
    for j in range(1, taps):
        total = total + picked[:, j * LANE : (j + 1) * LANE].reshape(
            parts * chans, rows, LANE
        ) * taps_ref[j]
    for c in range(chans):
        real = mr_ref[c, 0] * total[0] - mi_ref[c, 0] * total[chans]
        imag = mr_ref[c, 0] * total[chans] + mi_ref[c, 0] * total[0]
        for d in range(1, chans):
            real = real + mr_ref[c, d] * total[d] - mi_ref[c, d] * total[chans + d]
            imag = imag + mr_ref[c, d] * total[chans + d] + mi_ref[c, d] * total[d]
        out_ref[0, c] = real.astype(out_ref.dtype)
        out_ref[1, c] = imag.astype(out_ref.dtype)


def migrate_mix(spectra, tail, onehot, taps_c, mr_c, mi_c, tiles, tail_shift):
    parts, chans, wide, _ = spectra.shape
    rows = min(LANE, wide)
    taps = taps_c.shape[0]
    block = (parts, chans, rows, LANE)
    return pl.pallas_call(
        migrate_mix_kernel,
        out_shape=jax.ShapeDtypeStruct((parts, chans, wide, tiles * LANE), jnp.bfloat16),
        grid=(tiles, wide // rows),
        in_specs=[
            pl.BlockSpec(block, lambda t, f: (0, 0, f, t)),
            pl.BlockSpec(block, lambda t, f: (0, 0, f, t + tail_shift)),
            pl.BlockSpec((1, 2 * LANE, taps * LANE), lambda t, f: (t, 0, 0)),
            pl.BlockSpec((taps, rows, 1), lambda t, f: (0, f, 0)),
            pl.BlockSpec((chans, chans, rows, 1), lambda t, f: (0, 0, f, 0)),
            pl.BlockSpec((chans, chans, rows, 1), lambda t, f: (0, 0, f, 0)),
        ],
        out_specs=pl.BlockSpec(block, lambda t, f: (0, 0, f, t)),
    )(spectra, tail, onehot, taps_c, mr_c, mi_c)


CHUNKS = 1


def compress_block(echoes, range_phase, dev_count):
    parts, channels, pulses, range_bins = echoes.shape
    second = range_bins // R1
    per_block = second // dev_count
    block = range_bins // dev_count
    cosine = jnp.cos(range_phase)
    sine = jnp.sin(range_phase)
    real_in = echoes[0].astype(jnp.float32)
    imag_in = echoes[1].astype(jnp.float32)
    spectrum = jnp.stack(
        [real_in * cosine - imag_in * sine, real_in * sine + imag_in * cosine]
    ).astype(jnp.bfloat16)
    spectrum = spectrum.reshape((2, channels, pulses, R1, second))
    section = apply_table(complex_table(R1, R1, R1, 1.0, 1.0), spectrum, 0, 3)
    twist_re, twist_im = phase_pair(R1, second, range_bins, 1.0, 1.0 / math.sqrt(range_bins))
    twist_re = twist_re[:, None, None, :]
    twist_im = twist_im[:, None, None, :]
    partial_terms = jnp.stack(
        [
            section[0] * twist_re - section[1] * twist_im,
            section[0] * twist_im + section[1] * twist_re,
        ]
    ).astype(jnp.bfloat16)
    partial_terms = partial_terms.transpose(0, 2, 3, 1, 4)
    second_table = complex_table(second, second, second, 1.0, 1.0).transpose(1, 0, 2, 3)
    second_table = second_table.reshape((dev_count, per_block, 2, 2, second))
    result = lax.dot_general(
        second_table, partial_terms, (((3, 4), (0, 4)), ((), ())), preferred_element_type=jnp.float32
    ).astype(jnp.bfloat16)
    return result.transpose(0, 2, 3, 4, 1, 5).reshape((dev_count, 2, channels, pulses, block))


def body(echoes, range_phase, offsets, tap_weights, channel_mix, azimuth_filter):
    dev_count = lax.axis_size("dev")
    parts, channels, pulses, range_bins = echoes.shape
    block = range_bins // dev_count
    group_pulses = dev_count * pulses
    wide = group_pulses + group_pulses // 2
    forward = complex_table(wide, wide, wide, -1.0, 1.0 / math.sqrt(wide))
    own_table = forward[:, :, :, :group_pulses].reshape((2, wide, 2, dev_count, pulses))
    next_table = forward[:, :, :, group_pulses:].reshape((2, wide, 2, dev_count // 2, pulses))
    dims = (((2, 3, 4), (1, 0, 3)), ((), ()))
    step = channels // CHUNKS
    pieces = []
    for chunk in range(CHUNKS):
        with jax.named_scope(f"c{chunk}"):
            result = compress_block(
                echoes[:, chunk * step : (chunk + 1) * step], range_phase, dev_count
            )
        with jax.named_scope(f"x{chunk}"):
            turned = lax.all_to_all(result, "dev", 0, 0, tiled=True)
        with jax.named_scope(f"p{chunk}"):
            following = shifted(turned[: dev_count // 2], "blk", -1)
            spectra = (
                lax.dot_general(own_table, turned, dims, preferred_element_type=jnp.float32)
                + lax.dot_general(next_table, following, dims, preferred_element_type=jnp.float32)
            ).astype(jnp.bfloat16)
            pieces.append(spectra.transpose(0, 2, 1, 3))
    spectra = jnp.concatenate(pieces, axis=1)
    mix_real = (
        azimuth_filter[0][:, None, :] * channel_mix[0]
        - azimuth_filter[1][:, None, :] * channel_mix[1]
    )
    mix_imag = (
        azimuth_filter[0][:, None, :] * channel_mix[1]
        + azimuth_filter[1][:, None, :] * channel_mix[0]
    )
    taps = tap_weights.shape[0]
    tiles = block // LANE
    rows = jnp.arange(LANE, dtype=jnp.int32)
    span = jnp.arange(2 * LANE, dtype=jnp.int32)
    tap_range = jnp.arange(taps, dtype=jnp.int32)
    target = rows[None, :] + offsets.astype(jnp.int32).reshape(tiles, LANE)
    onehot = (
        span[None, :, None, None] == target[:, None, None, :] + tap_range[None, None, :, None]
    ).astype(jnp.bfloat16).reshape(tiles, 2 * LANE, taps * LANE)
    taps_c = tap_weights[:, :, None]
    mr_c = mix_real[:, :, :, None]
    mi_c = mix_imag[:, :, :, None]
    border = shifted(spectra[:, :, :, :LANE], "dev", -1)
    head = migrate_mix(spectra, spectra, onehot, taps_c, mr_c, mi_c, tiles - 1, 1)
    last = migrate_mix(
        spectra[:, :, :, block - LANE :], border, onehot[tiles - 1 :], taps_c, mr_c, mi_c, 1, 0
    )
    focused = jnp.concatenate([head, last], axis=3)
    backward = complex_table(group_pulses, wide, wide, 1.0, 1.0 / math.sqrt(wide))
    image = apply_table(backward, focused, 0, 2).astype(jnp.bfloat16)
    return image.transpose(0, 2, 1, 3)


def solution(mesh):
    in_specs = (P(None, None, ("blk", "dev"), None), P(), P("dev"), P(), P(), P())
    out_specs = P(None, None, "blk", "dev")
    return jax.shard_map(body, mesh=mesh, in_specs=in_specs, out_specs=out_specs, check_vma=False)
```

```python
import math

import jax
import jax.numpy as jnp
from jax import lax
from jax.experimental import pallas as pl
from jax.sharding import PartitionSpec as P


R1 = 128


def shifted(block, axis, distance):
    devices = range(lax.axis_size(axis))
    route = [(i - distance, i) for i in devices if i - distance in devices]
    return lax.ppermute(block, axis, route)


def phase_pair(row_count, col_count, length, direction, factor):
    product = (
        jnp.arange(row_count, dtype=jnp.int32)[:, None]
        * jnp.arange(col_count, dtype=jnp.int32)[None, :]
        % length
    )
    angle = product.astype(jnp.float32) * (direction * 2.0 * math.pi / length)
    return (jnp.cos(angle) * factor, jnp.sin(angle) * factor)


def complex_table(row_count, col_count, length, direction, factor):
    cosine, sine = phase_pair(row_count, col_count, length, direction, factor)
    upper = jnp.stack([cosine, -sine], axis=1)
    lower = jnp.stack([sine, cosine], axis=1)
    return jnp.stack([upper, lower]).astype(jnp.bfloat16)


def apply_table(table, data, part_dim, index_dim):
    return lax.dot_general(
        table, data, (((2, 3), (part_dim, index_dim)), ((), ())), preferred_element_type=jnp.float32
    )


LANE = 128


def migrate_mix_kernel(lead_ref, tail_ref, onehot_ref, taps_ref, mr_ref, mi_ref, out_ref):
    parts, chans, rows, _ = lead_ref.shape
    taps = taps_ref.shape[0]
    stack = parts * chans * rows
    window = jnp.concatenate(
        [lead_ref[...].reshape(stack, LANE), tail_ref[...].reshape(stack, LANE)], axis=1
    )
    picked = jnp.dot(window, onehot_ref[0], preferred_element_type=jnp.float32)
    total = picked[:, :LANE].reshape(parts * chans, rows, LANE) * taps_ref[0]
    for j in range(1, taps):
        total = total + picked[:, j * LANE : (j + 1) * LANE].reshape(
            parts * chans, rows, LANE
        ) * taps_ref[j]
    for c in range(chans):
        real = mr_ref[c, 0] * total[0] - mi_ref[c, 0] * total[chans]
        imag = mr_ref[c, 0] * total[chans] + mi_ref[c, 0] * total[0]
        for d in range(1, chans):
            real = real + mr_ref[c, d] * total[d] - mi_ref[c, d] * total[chans + d]
            imag = imag + mr_ref[c, d] * total[chans + d] + mi_ref[c, d] * total[d]
        out_ref[0, c] = real.astype(out_ref.dtype)
        out_ref[1, c] = imag.astype(out_ref.dtype)


def migrate_mix(spectra, tail, onehot, taps_c, mr_c, mi_c, tiles, tail_shift):
    parts, chans, wide, _ = spectra.shape
    rows = min(LANE, wide)
    taps = taps_c.shape[0]
    block = (parts, chans, rows, LANE)
    return pl.pallas_call(
        migrate_mix_kernel,
        out_shape=jax.ShapeDtypeStruct((parts, chans, wide, tiles * LANE), jnp.bfloat16),
        grid=(tiles, wide // rows),
        in_specs=[
            pl.BlockSpec(block, lambda t, f: (0, 0, f, t)),
            pl.BlockSpec(block, lambda t, f: (0, 0, f, t + tail_shift)),
            pl.BlockSpec((1, 2 * LANE, taps * LANE), lambda t, f: (t, 0, 0)),
            pl.BlockSpec((taps, rows, 1), lambda t, f: (0, f, 0)),
            pl.BlockSpec((chans, chans, rows, 1), lambda t, f: (0, 0, f, 0)),
            pl.BlockSpec((chans, chans, rows, 1), lambda t, f: (0, 0, f, 0)),
        ],
        out_specs=pl.BlockSpec(block, lambda t, f: (0, 0, f, t)),
    )(spectra, tail, onehot, taps_c, mr_c, mi_c)


CHUNKS = 1


def compress_block(echoes, range_phase, dev_count):
    _, channels, pulses, range_bins = echoes.shape
    second = range_bins // R1
    per_block = second // dev_count
    block = range_bins // dev_count
    cosine = jnp.cos(range_phase)
    sine = jnp.sin(range_phase)
    real_in = echoes[0].astype(jnp.float32)
    imag_in = echoes[1].astype(jnp.float32)
    spectrum = jnp.stack(
        [real_in * cosine - imag_in * sine, real_in * sine + imag_in * cosine]
    ).astype(jnp.bfloat16)
    spectrum = spectrum.reshape((2, channels, pulses, R1, second))
    section = apply_table(complex_table(R1, R1, R1, 1.0, 1.0), spectrum, 0, 3)
    twist_re, twist_im = phase_pair(R1, second, range_bins, 1.0, 1.0 / math.sqrt(range_bins))
    twist_re = twist_re[:, None, None, :]
    twist_im = twist_im[:, None, None, :]
    partial_terms = jnp.stack(
        [
            section[0] * twist_re - section[1] * twist_im,
            section[0] * twist_im + section[1] * twist_re,
        ]
    ).astype(jnp.bfloat16)
    partial_terms = partial_terms.transpose(0, 2, 3, 1, 4)
    second_table = complex_table(second, second, second, 1.0, 1.0).transpose(1, 0, 2, 3)
    second_table = second_table.reshape((dev_count, per_block, 2, 2, second))
    result = lax.dot_general(
        second_table, partial_terms, (((3, 4), (0, 4)), ((), ())), preferred_element_type=jnp.float32
    ).astype(jnp.bfloat16)
    return result.transpose(0, 2, 3, 4, 1, 5).reshape((dev_count, 2, channels, pulses, block))


def body(echoes, range_phase, offsets, tap_weights, channel_mix, azimuth_filter):
    dev_count = lax.axis_size("dev")
    _, channels, pulses, range_bins = echoes.shape
    block = range_bins // dev_count
    group_pulses = dev_count * pulses
    wide = group_pulses + group_pulses // 2
    forward = complex_table(wide, wide, wide, -1.0, 1.0 / math.sqrt(wide))
    own_table = forward[:, :, :, :group_pulses].reshape((2, wide, 2, dev_count, pulses))
    next_table = forward[:, :, :, group_pulses:].reshape((2, wide, 2, dev_count // 2, pulses))
    dims = (((2, 3, 4), (1, 0, 3)), ((), ()))
    step = channels // CHUNKS
    pieces = []
    for chunk in range(CHUNKS):
        result = compress_block(
            echoes[:, chunk * step : (chunk + 1) * step], range_phase, dev_count
        )
        turned = lax.all_to_all(result, "dev", 0, 0, tiled=True)
        following = shifted(turned[: dev_count // 2], "blk", -1)
        spectra = (
            lax.dot_general(own_table, turned, dims, preferred_element_type=jnp.float32)
            + lax.dot_general(next_table, following, dims, preferred_element_type=jnp.float32)
        ).astype(jnp.bfloat16)
        pieces.append(spectra.transpose(0, 2, 1, 3))
    spectra = jnp.concatenate(pieces, axis=1)
    mix_real = (
        azimuth_filter[0][:, None, :] * channel_mix[0]
        - azimuth_filter[1][:, None, :] * channel_mix[1]
    )
    mix_imag = (
        azimuth_filter[0][:, None, :] * channel_mix[1]
        + azimuth_filter[1][:, None, :] * channel_mix[0]
    )
    taps = tap_weights.shape[0]
    tiles = block // LANE
    rows = jnp.arange(LANE, dtype=jnp.int32)
    span = jnp.arange(2 * LANE, dtype=jnp.int32)
    tap_range = jnp.arange(taps, dtype=jnp.int32)
    target = rows[None, :] + offsets.astype(jnp.int32).reshape(tiles, LANE)
    onehot = (
        span[None, :, None, None] == target[:, None, None, :] + tap_range[None, None, :, None]
    ).astype(jnp.bfloat16).reshape(tiles, 2 * LANE, taps * LANE)
    taps_c = tap_weights[:, :, None]
    mr_c = mix_real[:, :, :, None]
    mi_c = mix_imag[:, :, :, None]
    border = shifted(spectra[:, :, :, :LANE], "dev", -1)
    head = migrate_mix(spectra, spectra, onehot, taps_c, mr_c, mi_c, tiles - 1, 1)
    last = migrate_mix(
        spectra[:, :, :, block - LANE :], border, onehot[tiles - 1 :], taps_c, mr_c, mi_c, 1, 0
    )
    focused = jnp.concatenate([head, last], axis=3)
    backward = complex_table(group_pulses, wide, wide, 1.0, 1.0 / math.sqrt(wide))
    image = apply_table(backward, focused, 0, 2).astype(jnp.bfloat16)
    return image.transpose(0, 2, 1, 3)


def solution(mesh):
    in_specs = (P(None, None, ("blk", "dev"), None), P(), P("dev"), P(), P(), P())
    out_specs = P(None, None, "blk", "dev")
    return jax.shard_map(body, mesh=mesh, in_specs=in_specs, out_specs=out_specs, check_vma=False)
```

```python
import math

import jax
import jax.numpy as jnp
from jax import lax
from jax.sharding import PartitionSpec as P


R1 = 128
MARG = 64


def shifted(block, axis, distance):
    devices = range(lax.axis_size(axis))
    route = [(i - distance, i) for i in devices if i - distance in devices]
    return lax.ppermute(block, axis, route)


def phase_pair(row_count, col_count, length, direction, factor):
    product = (
        jnp.arange(row_count, dtype=jnp.int32)[:, None]
        * jnp.arange(col_count, dtype=jnp.int32)[None, :]
        % length
    )
    angle = product.astype(jnp.float32) * (direction * 2.0 * math.pi / length)
    return (jnp.cos(angle) * factor, jnp.sin(angle) * factor)


def complex_table(row_count, col_count, length, direction, factor):
    cosine, sine = phase_pair(row_count, col_count, length, direction, factor)
    upper = jnp.stack([cosine, -sine], axis=1)
    lower = jnp.stack([sine, cosine], axis=1)
    return jnp.stack([upper, lower]).astype(jnp.bfloat16)


def apply_table(table, data, part_dim, index_dim):
    return lax.dot_general(
        table, data, (((2, 3), (part_dim, index_dim)), ((), ())), preferred_element_type=jnp.float32
    )


def migrate(spectra, border, offsets, tap_weights, block):
    tile = min(128, block)
    taps = tap_weights.shape[0]
    pieces = []
    for tile_index in range(block // tile):
        first = tile_index * tile
        rows_here = jnp.arange(tile, dtype=jnp.int32)
        target = rows_here + offsets[first : first + tile]
        columns = jnp.arange(tile + MARG, dtype=jnp.int32)
        tap_range = jnp.arange(taps, dtype=jnp.int32)
        onehot = (
            columns[None, None, :] == target[None, :, None] + tap_range[:, None, None]
        ).astype(jnp.bfloat16)
        if first + tile + MARG <= block:
            window_part = spectra[:, :, :, first : first + tile + MARG]
        else:
            window_part = jnp.concatenate(
                [spectra[:, :, :, first:], border[:, :, :, :MARG]], axis=3
            )
        picked = lax.dot_general(
            window_part, onehot, (((3,), (2,)), ((), ())), preferred_element_type=jnp.bfloat16
        )
        total = jnp.zeros(picked.shape[:3] + (tile,), jnp.float32)
        for tap_index in range(taps):
            total = total + picked[:, :, :, tap_index].astype(jnp.float32) * tap_weights[
                tap_index
            ][None, :, None, None]
        pieces.append(total)
    return jnp.concatenate(pieces, axis=3)


CHUNKS = 1


def compress_block(echoes, range_phase, dev_count):
    _, channels, pulses, range_bins = echoes.shape
    second = range_bins // R1
    per_block = second // dev_count
    block = range_bins // dev_count
    cosine = jnp.cos(range_phase)
    sine = jnp.sin(range_phase)
    real_in = echoes[0].astype(jnp.float32)
    imag_in = echoes[1].astype(jnp.float32)
    spectrum = jnp.stack(
        [real_in * cosine - imag_in * sine, real_in * sine + imag_in * cosine]
    ).astype(jnp.bfloat16)
    spectrum = spectrum.reshape((2, channels, pulses, R1, second))
    section = apply_table(complex_table(R1, R1, R1, 1.0, 1.0), spectrum, 0, 3)
    twist_re, twist_im = phase_pair(R1, second, range_bins, 1.0, 1.0 / math.sqrt(range_bins))
    twist_re = twist_re[:, None, None, :]
    twist_im = twist_im[:, None, None, :]
    partial_terms = jnp.stack(
        [
            section[0] * twist_re - section[1] * twist_im,
            section[0] * twist_im + section[1] * twist_re,
        ]
    ).astype(jnp.bfloat16)
    partial_terms = partial_terms.transpose(0, 2, 3, 1, 4)
    second_table = complex_table(second, second, second, 1.0, 1.0).transpose(1, 0, 2, 3)
    second_table = second_table.reshape((dev_count, per_block, 2, 2, second))
    result = lax.dot_general(
        second_table, partial_terms, (((3, 4), (0, 4)), ((), ())), preferred_element_type=jnp.float32
    ).astype(jnp.bfloat16)
    return result.transpose(0, 2, 3, 4, 1, 5).reshape((dev_count, 2, channels, pulses, block))


def body(echoes, range_phase, offsets, tap_weights, channel_mix, azimuth_filter):
    dev_count = lax.axis_size("dev")
    _, channels, pulses, range_bins = echoes.shape
    block = range_bins // dev_count
    group_pulses = dev_count * pulses
    wide = group_pulses + group_pulses // 2
    forward = complex_table(wide, wide, wide, -1.0, 1.0 / math.sqrt(wide))
    own_table = forward[:, :, :, :group_pulses].reshape((2, wide, 2, dev_count, pulses))
    next_table = forward[:, :, :, group_pulses:].reshape((2, wide, 2, dev_count // 2, pulses))
    dims = (((2, 3, 4), (1, 0, 3)), ((), ()))
    step = channels // CHUNKS
    pieces = []
    for chunk in range(CHUNKS):
        result = compress_block(
            echoes[:, chunk * step : (chunk + 1) * step], range_phase, dev_count
        )
        turned = lax.all_to_all(result, "dev", 0, 0, tiled=True)
        following = shifted(turned[: dev_count // 2], "blk", -1)
        spectra = (
            lax.dot_general(own_table, turned, dims, preferred_element_type=jnp.float32)
            + lax.dot_general(next_table, following, dims, preferred_element_type=jnp.float32)
        ).astype(jnp.bfloat16)
        border = shifted(spectra[:, :, :, : 2 * MARG], "dev", -1)
        pieces.append(migrate(spectra, border, offsets, tap_weights, block))
    moved = jnp.concatenate(pieces, axis=2)
    mix_real = (
        azimuth_filter[0][:, None, :] * channel_mix[0]
        - azimuth_filter[1][:, None, :] * channel_mix[1]
    )
    mix_imag = (
        azimuth_filter[0][:, None, :] * channel_mix[1]
        + azimuth_filter[1][:, None, :] * channel_mix[0]
    )
    rows_real = []
    rows_imag = []
    for channel in range(channels):
        sum_real = jnp.zeros((wide, block), jnp.float32)
        sum_imag = jnp.zeros((wide, block), jnp.float32)
        for other_chan in range(channels):
            coef_real = mix_real[channel, other_chan][:, None]
            coef_imag = mix_imag[channel, other_chan][:, None]
            sum_real = (
                sum_real + coef_real * moved[0, :, other_chan] - coef_imag * moved[1, :, other_chan]
            )
            sum_imag = (
                sum_imag + coef_real * moved[1, :, other_chan] + coef_imag * moved[0, :, other_chan]
            )
        rows_real.append(sum_real)
        rows_imag.append(sum_imag)
    focused = jnp.stack([jnp.stack(rows_real, axis=1), jnp.stack(rows_imag, axis=1)]).astype(
        jnp.bfloat16
    )
    backward = complex_table(group_pulses, wide, wide, 1.0, 1.0 / math.sqrt(wide))
    image = apply_table(backward, focused, 0, 1).astype(jnp.bfloat16)
    return image.transpose(0, 2, 1, 3)


def solution(mesh):
    in_specs = (P(None, None, ("blk", "dev"), None), P(), P("dev"), P(), P(), P())
    out_specs = P(None, None, "blk", "dev")
    return jax.shard_map(body, mesh=mesh, in_specs=in_specs, out_specs=out_specs, check_vma=False)
```

```python
import math

import jax
import jax.numpy as jnp
from jax import lax
from jax.sharding import PartitionSpec as P


R1 = 128
MARG = 64


def shifted(block, axis, distance):
    devices = range(lax.axis_size(axis))
    route = [(i - distance, i) for i in devices if i - distance in devices]
    return lax.ppermute(block, axis, route)


def phase_pair(row_count, col_count, length, direction, factor):
    product = (
        jnp.arange(row_count, dtype=jnp.int32)[:, None]
        * jnp.arange(col_count, dtype=jnp.int32)[None, :]
        % length
    )
    angle = product.astype(jnp.float32) * (direction * 2.0 * math.pi / length)
    return (jnp.cos(angle) * factor, jnp.sin(angle) * factor)


def complex_table(row_count, col_count, length, direction, factor):
    cosine, sine = phase_pair(row_count, col_count, length, direction, factor)
    upper = jnp.stack([cosine, -sine], axis=1)
    lower = jnp.stack([sine, cosine], axis=1)
    return jnp.stack([upper, lower]).astype(jnp.bfloat16)


def apply_table(table, data, part_dim, index_dim):
    return lax.dot_general(
        table, data, (((2, 3), (part_dim, index_dim)), ((), ())), preferred_element_type=jnp.float32
    )


def migrate(window, offsets, tap_weights, block):
    tile = min(128, block)
    taps = tap_weights.shape[0]
    pieces = []
    for tile_index in range(block // tile):
        first = tile_index * tile
        rows_here = jnp.arange(tile, dtype=jnp.int32)
        target = rows_here + offsets[first : first + tile]
        columns = jnp.arange(tile + MARG, dtype=jnp.int32)
        tap_range = jnp.arange(taps, dtype=jnp.int32)
        onehot = (
            columns[None, None, :] == target[None, :, None] + tap_range[:, None, None]
        ).astype(jnp.bfloat16)
        window_part = window(first, first + tile + MARG)
        picked = lax.dot_general(
            window_part, onehot, (((3,), (2,)), ((), ())), preferred_element_type=jnp.bfloat16
        )
        total = jnp.zeros(picked.shape[:3] + (tile,), jnp.float32)
        for tap_index in range(taps):
            total = total + picked[:, :, :, tap_index].astype(jnp.float32) * tap_weights[
                tap_index
            ][None, :, None, None]
        pieces.append(total)
    return jnp.concatenate(pieces, axis=3)


CHUNKS = 1


def compress_block(echoes, range_phase, dev_count):
    _, channels, pulses, range_bins = echoes.shape
    second = range_bins // R1
    per_block = second // dev_count
    block = range_bins // dev_count
    cosine = jnp.cos(range_phase)
    sine = jnp.sin(range_phase)
    real_in = echoes[0].astype(jnp.float32)
    imag_in = echoes[1].astype(jnp.float32)
    spectrum = jnp.stack(
        [real_in * cosine - imag_in * sine, real_in * sine + imag_in * cosine]
    ).astype(jnp.bfloat16)
    spectrum = spectrum.reshape((2, channels, pulses, R1, second))
    section = apply_table(complex_table(R1, R1, R1, 1.0, 1.0), spectrum, 0, 3)
    twist_re, twist_im = phase_pair(R1, second, range_bins, 1.0, 1.0 / math.sqrt(range_bins))
    twist_re = twist_re[:, None, None, :]
    twist_im = twist_im[:, None, None, :]
    partial_terms = jnp.stack(
        [
            section[0] * twist_re - section[1] * twist_im,
            section[0] * twist_im + section[1] * twist_re,
        ]
    ).astype(jnp.bfloat16)
    partial_terms = partial_terms.transpose(0, 2, 3, 1, 4)
    second_table = complex_table(second, second, second, 1.0, 1.0).transpose(1, 0, 2, 3)
    second_table = second_table.reshape((dev_count, per_block, 2, 2, second))
    result = lax.dot_general(
        second_table, partial_terms, (((3, 4), (0, 4)), ((), ())), preferred_element_type=jnp.float32
    ).astype(jnp.bfloat16)
    return result.transpose(0, 2, 3, 4, 1, 5).reshape((dev_count, 2, channels, pulses, block))


def body(echoes, range_phase, offsets, tap_weights, channel_mix, azimuth_filter):
    dev_count = lax.axis_size("dev")
    _, channels, pulses, range_bins = echoes.shape
    block = range_bins // dev_count
    group_pulses = dev_count * pulses
    wide = group_pulses + group_pulses // 2
    forward = complex_table(wide, wide, wide, -1.0, 1.0 / math.sqrt(wide))
    own_table = forward[:, :, :, :group_pulses].reshape((2, wide, 2, dev_count, pulses))
    next_table = forward[:, :, :, group_pulses:].reshape((2, wide, 2, dev_count // 2, pulses))
    dims = (((2, 3, 4), (1, 0, 3)), ((), ()))
    step = channels // CHUNKS
    pieces = []
    for chunk in range(CHUNKS):
        result = compress_block(
            echoes[:, chunk * step : (chunk + 1) * step], range_phase, dev_count
        )
        turned = lax.all_to_all(result, "dev", 0, 0, tiled=True)
        following = shifted(turned[: dev_count // 2], "blk", -1)
        lead_width = 2 * MARG
        head = (
            lax.dot_general(
                own_table, turned[..., :lead_width], dims, preferred_element_type=jnp.float32
            )
            + lax.dot_general(
                next_table, following[..., :lead_width], dims, preferred_element_type=jnp.float32
            )
        ).astype(jnp.bfloat16)
        border = shifted(head, "dev", -1)
        rest = (
            lax.dot_general(
                own_table, turned[..., lead_width:], dims, preferred_element_type=jnp.float32
            )
            + lax.dot_general(
                next_table,
                following[..., lead_width:],
                dims,
                preferred_element_type=jnp.float32,
            )
        ).astype(jnp.bfloat16)

        def window(low, high):
            spans = ((head, 0), (rest, lead_width), (border[..., :MARG], block))
            parts = []
            for piece, start in spans:
                lo = max(low, start)
                hi = min(high, start + piece.shape[3])
                if lo < hi:
                    parts.append(piece[..., lo - start : hi - start])
            return parts[0] if len(parts) == 1 else jnp.concatenate(parts, axis=3)

        pieces.append(migrate(window, offsets, tap_weights, block))
    moved = jnp.concatenate(pieces, axis=2)
    mix_real = (
        azimuth_filter[0][:, None, :] * channel_mix[0]
        - azimuth_filter[1][:, None, :] * channel_mix[1]
    )
    mix_imag = (
        azimuth_filter[0][:, None, :] * channel_mix[1]
        + azimuth_filter[1][:, None, :] * channel_mix[0]
    )
    rows_real = []
    rows_imag = []
    for channel in range(channels):
        sum_real = jnp.zeros((wide, block), jnp.float32)
        sum_imag = jnp.zeros((wide, block), jnp.float32)
        for other_chan in range(channels):
            coef_real = mix_real[channel, other_chan][:, None]
            coef_imag = mix_imag[channel, other_chan][:, None]
            sum_real = (
                sum_real + coef_real * moved[0, :, other_chan] - coef_imag * moved[1, :, other_chan]
            )
            sum_imag = (
                sum_imag + coef_real * moved[1, :, other_chan] + coef_imag * moved[0, :, other_chan]
            )
        rows_real.append(sum_real)
        rows_imag.append(sum_imag)
    focused = jnp.stack([jnp.stack(rows_real, axis=1), jnp.stack(rows_imag, axis=1)]).astype(
        jnp.bfloat16
    )
    backward = complex_table(group_pulses, wide, wide, 1.0, 1.0 / math.sqrt(wide))
    image = apply_table(backward, focused, 0, 1).astype(jnp.bfloat16)
    return image.transpose(0, 2, 1, 3)


def solution(mesh):
    in_specs = (P(None, None, ("blk", "dev"), None), P(), P("dev"), P(), P(), P())
    out_specs = P(None, None, "blk", "dev")
    return jax.shard_map(body, mesh=mesh, in_specs=in_specs, out_specs=out_specs, check_vma=False)
```

```python
import math

import jax
import jax.numpy as jnp
from jax import lax
from jax.sharding import PartitionSpec as P


R1 = 128
MARG = 64


def shifted(block, axis, distance):
    devices = range(lax.axis_size(axis))
    route = [(i - distance, i) for i in devices if i - distance in devices]
    return lax.ppermute(block, axis, route)


def phase_pair(row_count, col_count, length, direction, factor):
    product = (
        jnp.arange(row_count, dtype=jnp.int32)[:, None]
        * jnp.arange(col_count, dtype=jnp.int32)[None, :]
        % length
    )
    angle = product.astype(jnp.float32) * (direction * 2.0 * math.pi / length)
    return (jnp.cos(angle) * factor, jnp.sin(angle) * factor)


def complex_table(row_count, col_count, length, direction, factor):
    cosine, sine = phase_pair(row_count, col_count, length, direction, factor)
    upper = jnp.stack([cosine, -sine], axis=1)
    lower = jnp.stack([sine, cosine], axis=1)
    return jnp.stack([upper, lower]).astype(jnp.bfloat16)


def apply_table(table, data, part_dim, index_dim):
    return lax.dot_general(
        table, data, (((2, 3), (part_dim, index_dim)), ((), ())), preferred_element_type=jnp.float32
    )


def migrate(window, offsets, tap_weights, block):
    tile = min(128, block)
    taps = tap_weights.shape[0]
    pieces = []
    for tile_index in range(block // tile):
        first = tile_index * tile
        rows_here = jnp.arange(tile, dtype=jnp.int32)
        target = rows_here + offsets[first : first + tile]
        columns = jnp.arange(tile + MARG, dtype=jnp.int32)
        tap_range = jnp.arange(taps, dtype=jnp.int32)
        onehot = (
            columns[None, None, :] == target[None, :, None] + tap_range[:, None, None]
        ).astype(jnp.bfloat16)
        window_part = window(first, first + tile + MARG)
        picked = lax.dot_general(
            window_part, onehot, (((3,), (2,)), ((), ())), preferred_element_type=jnp.bfloat16
        )
        total = jnp.zeros(picked.shape[:3] + (tile,), jnp.float32)
        for tap_index in range(taps):
            total = total + picked[:, :, :, tap_index].astype(jnp.float32) * tap_weights[
                tap_index
            ][None, :, None, None]
        pieces.append(total)
    return pieces


CHUNKS = 1


def compress_block(echoes, range_phase, dev_count):
    _, channels, pulses, range_bins = echoes.shape
    second = range_bins // R1
    per_block = second // dev_count
    block = range_bins // dev_count
    cosine = jnp.cos(range_phase)
    sine = jnp.sin(range_phase)
    real_in = echoes[0].astype(jnp.float32)
    imag_in = echoes[1].astype(jnp.float32)
    spectrum = jnp.stack(
        [real_in * cosine - imag_in * sine, real_in * sine + imag_in * cosine]
    ).astype(jnp.bfloat16)
    spectrum = spectrum.reshape((2, channels, pulses, R1, second))
    section = apply_table(complex_table(R1, R1, R1, 1.0, 1.0), spectrum, 0, 3)
    twist_re, twist_im = phase_pair(R1, second, range_bins, 1.0, 1.0 / math.sqrt(range_bins))
    twist_re = twist_re[:, None, None, :]
    twist_im = twist_im[:, None, None, :]
    partial_terms = jnp.stack(
        [
            section[0] * twist_re - section[1] * twist_im,
            section[0] * twist_im + section[1] * twist_re,
        ]
    ).astype(jnp.bfloat16)
    partial_terms = partial_terms.transpose(0, 2, 3, 1, 4)
    second_table = complex_table(second, second, second, 1.0, 1.0).transpose(1, 0, 2, 3)
    second_table = second_table.reshape((dev_count, per_block, 2, 2, second))
    result = lax.dot_general(
        second_table, partial_terms, (((3, 4), (0, 4)), ((), ())), preferred_element_type=jnp.float32
    ).astype(jnp.bfloat16)
    return result.transpose(0, 2, 3, 4, 1, 5).reshape((dev_count, 2, channels, pulses, block))


def body(echoes, range_phase, offsets, tap_weights, channel_mix, azimuth_filter):
    dev_count = lax.axis_size("dev")
    _, channels, pulses, range_bins = echoes.shape
    block = range_bins // dev_count
    group_pulses = dev_count * pulses
    wide = group_pulses + group_pulses // 2
    forward = complex_table(wide, wide, wide, -1.0, 1.0 / math.sqrt(wide))
    own_table = forward[:, :, :, :group_pulses].reshape((2, wide, 2, dev_count, pulses))
    next_table = forward[:, :, :, group_pulses:].reshape((2, wide, 2, dev_count // 2, pulses))
    dims = (((2, 3, 4), (1, 0, 3)), ((), ()))
    step = channels // CHUNKS
    pieces = []
    for chunk in range(CHUNKS):
        result = compress_block(
            echoes[:, chunk * step : (chunk + 1) * step], range_phase, dev_count
        )
        turned = lax.all_to_all(result, "dev", 0, 0, tiled=True)
        following = shifted(turned[: dev_count // 2], "blk", -1)
        lead_width = 2 * MARG
        head = (
            lax.dot_general(
                own_table, turned[..., :lead_width], dims, preferred_element_type=jnp.float32
            )
            + lax.dot_general(
                next_table, following[..., :lead_width], dims, preferred_element_type=jnp.float32
            )
        ).astype(jnp.bfloat16)
        border = shifted(head, "dev", -1)
        rest = (
            lax.dot_general(
                own_table, turned[..., lead_width:], dims, preferred_element_type=jnp.float32
            )
            + lax.dot_general(
                next_table,
                following[..., lead_width:],
                dims,
                preferred_element_type=jnp.float32,
            )
        ).astype(jnp.bfloat16)

        def window(low, high):
            spans = ((head, 0), (rest, lead_width), (border[..., :MARG], block))
            parts = []
            for piece, start in spans:
                lo = max(low, start)
                hi = min(high, start + piece.shape[3])
                if lo < hi:
                    parts.append(piece[..., lo - start : hi - start])
            return parts[0] if len(parts) == 1 else jnp.concatenate(parts, axis=3)

        pieces.append(migrate(window, offsets, tap_weights, block))
    tiles_moved = [jnp.concatenate(group, axis=2) for group in zip(*pieces)]
    mix_real = (
        azimuth_filter[0][:, None, :] * channel_mix[0]
        - azimuth_filter[1][:, None, :] * channel_mix[1]
    )
    mix_imag = (
        azimuth_filter[0][:, None, :] * channel_mix[1]
        + azimuth_filter[1][:, None, :] * channel_mix[0]
    )
    focused_tiles = []
    for moved in tiles_moved:
        width = moved.shape[3]
        rows_real = []
        rows_imag = []
        for channel in range(channels):
            sum_real = jnp.zeros((wide, width), jnp.float32)
            sum_imag = jnp.zeros((wide, width), jnp.float32)
            for other_chan in range(channels):
                coef_real = mix_real[channel, other_chan][:, None]
                coef_imag = mix_imag[channel, other_chan][:, None]
                sum_real = (
                    sum_real
                    + coef_real * moved[0, :, other_chan]
                    - coef_imag * moved[1, :, other_chan]
                )
                sum_imag = (
                    sum_imag
                    + coef_real * moved[1, :, other_chan]
                    + coef_imag * moved[0, :, other_chan]
                )
            rows_real.append(sum_real)
            rows_imag.append(sum_imag)
        focused_tiles.append(
            jnp.stack([jnp.stack(rows_real, axis=1), jnp.stack(rows_imag, axis=1)]).astype(
                jnp.bfloat16
            )
        )
    focused = jnp.concatenate(focused_tiles, axis=3)
    backward = complex_table(group_pulses, wide, wide, 1.0, 1.0 / math.sqrt(wide))
    image = apply_table(backward, focused, 0, 1).astype(jnp.bfloat16)
    return image.transpose(0, 2, 1, 3)


def solution(mesh):
    in_specs = (P(None, None, ("blk", "dev"), None), P(), P("dev"), P(), P(), P())
    out_specs = P(None, None, "blk", "dev")
    return jax.shard_map(body, mesh=mesh, in_specs=in_specs, out_specs=out_specs, check_vma=False)
```
